32 devices in a mesh: req: 8 (over y, x, core), kv: 4 (over z).
Axes of the slice: x: 2, y: 2, z: 4, core: 2. Of those that a mesh axis runs over, the one named last changes fastest.
Arguments:
- hidden: bfloat16 [128, 8192], P('req', 'kv')
- cache_len: int32 [2, 128], replicated, may hold values from 1 to 4096, as said below
- request_serving_order: int32 [128], replicated, may hold values from 0 to 127, as said below
- rotated_key_cache: bfloat16 [2, 65536, 1024], P(None, 'req', 'kv'), as said below
- stored_value_cache: bfloat16 [2, 65536, 1024], P(None, 'req', 'kv'), may hold values from -6 to 6
- attn_gain: bfloat16 [8192], P('kv'), may hold values from 0.099609375 to 1.8984375
- w_query: bfloat16 [8192, 8192], P('req', 'kv'), may hold values from -0.0625 to 0.0625
- key_projection_weight: bfloat16 [8192, 1024], P('req', 'kv'), may hold values from -0.0625 to 0.0625
- value_projection_weight: bfloat16 [8192, 1024], P('req', 'kv'), may hold values from -0.0625 to 0.0625
- b_query: bfloat16 [8192], P('kv'), may hold values from -3 to 3
- key_bias: bfloat16 [1024], P('kv'), may hold values from -4.5 to 4.5
- value_bias: bfloat16 [1024], P('kv'), may hold values from -4.5 to 4.5
- w_out: bfloat16 [8192, 8192], P('req', 'kv'), may hold values from -0.0625 to 0.0625
- mlp_gain: bfloat16 [8192], P('kv'), may hold values from 0.099609375 to 1.8984375
- w_gate: bfloat16 [8192, 29568], P('kv', 'req'), may hold values from -0.0625 to 0.0625
- w_up: bfloat16 [8192, 29568], P('kv', 'req'), may hold values from -0.0625 to 0.0625
- w_down: bfloat16 [29568, 8192], P('req', 'kv'), may hold values from -0.03125 to 0.03125
Outputs:
- residual: float32 [128, 8192], P('req', 'kv')
The draws below stay inside these ranges and needn't reach their ends.
Inputs may be any that keep to these rules, and one draw needn't show every extreme that they name: `request_serving_order`: A permutation of the requests. `cache_len`: in each layer the caches of the requests of one serving index of req sum to at most 8192 rows, and to exactly 8192 for one index; some request of that index has exactly 4096. `rotated_key_cache`: rows of an index beyond its requests' caches hold no cached tokens.
All inputs are finite; a program needn't handle non-finite values.
Results may differ from the reference program's by a relative error of at most 0.015.
Values may be sent and summed in bfloat16 or wider, within the bound.
No kernel may reach another device: no remote copies, remote signals or barrier semaphores. Data moves between devices by JAX's collectives and lax.ppermute only.
A program may use at most 256 MiB of HBM per device.

```python
import math
import jax
import jax.numpy as jnp
from jax import lax

MODEL_WIDTH = 8192
QUERY_HEADS = 64
KEY_VALUE_HEADS = 8
HEAD_SIZE = 128
FF = 29568
REQUESTS_PER_IDX = 16
LAYER_COUNT = 2
REQUEST_TOTAL = 128
SLOT_CAPACITY = 8192
MAXLEN = 4096
N_REQ = 8


def deal_and_lengths(key):
    key_perm, key_heavy, key_total, key_weight = jax.random.split(jax.random.fold_in(key, 11), 4)
    request_serving_order = jax.random.permutation(key_perm, REQUEST_TOTAL).astype(jnp.int32)
    heavy_index = jax.random.randint(key_heavy, (LAYER_COUNT, 1), 0, N_REQ)
    totals = jax.random.randint(key_total, (LAYER_COUNT, N_REQ), SLOT_CAPACITY // 4, SLOT_CAPACITY * 3 // 4 + 1)
    weights = jax.random.randint(key_weight, (LAYER_COUNT, N_REQ, REQUESTS_PER_IDX), 16, 49)
    device_ids = jnp.arange(N_REQ, dtype=jnp.int32)[None, :]
    is_heavy = (device_ids == heavy_index)[:, :, None]
    slot_ids = jnp.arange(REQUESTS_PER_IDX, dtype=jnp.int32)[None, None, :]
    reserved = is_heavy & (slot_ids == 0)
    free_weights = jnp.where(reserved, 0, weights)
    weight_sum = jnp.sum(free_weights, axis=2, keepdims=True)
    free_count = jnp.where(is_heavy, REQUESTS_PER_IDX - 1, REQUESTS_PER_IDX)
    free_total = jnp.where(is_heavy, SLOT_CAPACITY - MAXLEN, totals[:, :, None])
    spare = free_total - free_count
    base_len = jnp.where(reserved, 0, 1 + spare * free_weights // weight_sum)
    remainder = free_total - jnp.sum(base_len, axis=2, keepdims=True)
    target_slot = jnp.where(is_heavy, 1, 0)
    base_len = base_len + jnp.where(slot_ids == target_slot, remainder, 0)
    slot_len = jnp.where(reserved, MAXLEN, base_len).reshape(LAYER_COUNT, REQUEST_TOTAL)
    inverse = jnp.argsort(request_serving_order)
    cache_len = jnp.take(slot_len, inverse, axis=1).astype(jnp.int32)
    return (request_serving_order, cache_len)


def draw_request_serving_order(key, part):
    return deal_and_lengths(key)[0]


def draw_cache_len(key, part):
    return deal_and_lengths(key)[1]


def draw_hidden(key, part):
    key_rows, key_cols, key_base = jax.random.split(jax.random.fold_in(key, 3), 3)
    row_scale = jnp.exp(jax.random.uniform(key_rows, (REQUEST_TOTAL, 1), jnp.float32, math.log(0.5), math.log(2.0)))
    jitter = jnp.exp(jax.random.uniform(key_cols, (1, MODEL_WIDTH), jnp.float32, math.log(0.7), math.log(1.4)))
    position = jnp.arange(MODEL_WIDTH, dtype=jnp.float32)[None, :] / (MODEL_WIDTH - 1)
    ramp = jnp.exp(math.log(0.35) + position * math.log(10.0))
    base_values = jax.random.normal(key_base, (REQUEST_TOTAL, MODEL_WIDTH), jnp.float32)
    return (base_values * row_scale * ramp * jitter).astype(jnp.bfloat16)


def draw_rotated_key_cache(key, part):
    key_base = jax.random.fold_in(jax.random.fold_in(key, 5), 0)
    gathered_shape = (LAYER_COUNT, N_REQ * SLOT_CAPACITY, KEY_VALUE_HEADS * HEAD_SIZE)
    base_values = 2.0 * jax.random.normal(key_base, gathered_shape, jnp.float32)
    return base_values.astype(jnp.bfloat16)


def block_scale(own_key, extent, cuts, least, top_value):
    level, own = 1.0, jax.random.fold_in(own_key, 6)
    for dim, shards_of in cuts:
        heights = jnp.exp(jax.random.uniform(jax.random.fold_in(own, dim), (shards_of,), jnp.float32, least / len(cuts), top_value / len(cuts)))
        level = level * jnp.repeat(heights, extent[dim] // shards_of).reshape([-1 if axis == dim else 1 for axis in range(len(extent))])
    return level


def centred(own_key, shape, spread, reach, pieces=(), kind=jnp.bfloat16):
    array = jax.random.normal(own_key, shape, jnp.float32) * spread
    if len(pieces) > 0:
        array = block_scale(own_key, shape, pieces, -0.22, 0.18) * array
    return jnp.clip(array, min=-reach, max=reach).astype(kind)


def setup_inputs(seed: int = 0) -> dict:
    key_list = jax.random.split(jax.random.key(seed), 18)
    hidden = draw_hidden(jax.random.fold_in(key_list[17], 71), 0)
    cache_len = draw_cache_len(jax.random.fold_in(key_list[17], 71), 0)
    request_serving_order = draw_request_serving_order(jax.random.fold_in(key_list[17], 71), 0)
    rotated_key_cache = draw_rotated_key_cache(jax.random.fold_in(key_list[17], 71), 0)
    stored_value_cache = centred(key_list[4], (LAYER_COUNT, N_REQ * SLOT_CAPACITY, KEY_VALUE_HEADS * HEAD_SIZE), 1.0, 6.0, ((1, 8), (2, 4)))
    attn_gain = jnp.clip(1.0 + 0.18 * jax.random.normal(key_list[5], (MODEL_WIDTH,), jnp.float32), 0.099609375, 1.8984375).astype(jnp.bfloat16)
    w_query = centred(key_list[6], (MODEL_WIDTH, QUERY_HEADS * HEAD_SIZE), MODEL_WIDTH ** -0.5, 0.0625, ((0, 8), (1, 4)))
    key_projection_weight = centred(key_list[7], (MODEL_WIDTH, KEY_VALUE_HEADS * HEAD_SIZE), MODEL_WIDTH ** -0.5, 0.0625, ((0, 8), (1, 4)))
    value_projection_weight = centred(key_list[8], (MODEL_WIDTH, KEY_VALUE_HEADS * HEAD_SIZE), MODEL_WIDTH ** -0.5, 0.0625, ((0, 8), (1, 4)))
    b_query = centred(key_list[9], (QUERY_HEADS * HEAD_SIZE,), 0.5, 3.0, ((0, 4),))
    key_bias = centred(key_list[10], (KEY_VALUE_HEADS * HEAD_SIZE,), 1.5, 4.5, ((0, 4),))
    value_bias = centred(key_list[11], (KEY_VALUE_HEADS * HEAD_SIZE,), 1.5, 4.5, ((0, 4),))
    w_out = centred(key_list[12], (QUERY_HEADS * HEAD_SIZE, MODEL_WIDTH), (QUERY_HEADS * HEAD_SIZE) ** -0.5, 0.0625, ((0, 8), (1, 4)))
    mlp_gain = jnp.clip(1.0 + 0.18 * jax.random.normal(key_list[13], (MODEL_WIDTH,), jnp.float32), 0.099609375, 1.8984375).astype(jnp.bfloat16)
    w_gate = centred(key_list[14], (MODEL_WIDTH, FF), MODEL_WIDTH ** -0.5, 0.0625, ((0, 4), (1, 8)))
    w_up = centred(key_list[15], (MODEL_WIDTH, FF), MODEL_WIDTH ** -0.5, 0.0625, ((0, 4), (1, 8)))
    w_down = centred(key_list[16], (FF, MODEL_WIDTH), FF ** -0.5, 0.03125, ((0, 8), (1, 4)))
    return {"hidden": hidden, "cache_len": cache_len, "request_serving_order": request_serving_order, "rotated_key_cache": rotated_key_cache, "stored_value_cache": stored_value_cache, "attn_gain": attn_gain, "w_query": w_query, "key_projection_weight": key_projection_weight, "value_projection_weight": value_projection_weight, "b_query": b_query, "key_bias": key_bias, "value_bias": value_bias, "w_out": w_out, "mlp_gain": mlp_gain, "w_gate": w_gate, "w_up": w_up, "w_down": w_down}


EPS = 1e-06
LOG_BASE = math.log(1000000.0)

def apply_rotation(values, token_positions):
    half_width = values.shape[-1] // 2
    frequency = jnp.exp(-LOG_BASE * jnp.arange(half_width, dtype=jnp.float32) * 2.0 / values.shape[-1])
    angles = token_positions[:, None] * frequency[None, :]
    reshape_to = (angles.shape[0],) + (1,) * (values.ndim - 2) + (half_width,)
    cosine = jnp.cos(angles).reshape(reshape_to)
    sine_part = jnp.sin(angles).reshape(reshape_to)
    front_half = values[..., :half_width]
    back_half = values[..., half_width:]
    return jnp.concatenate([front_half * cosine - back_half * sine_part, back_half * cosine + front_half * sine_part], axis=-1)

def normalize(residual, gains):
    inv_norm = lax.rsqrt(lax.optimization_barrier(jnp.sum(residual * residual, axis=1, keepdims=True)) / MODEL_WIDTH + EPS)
    return (residual * inv_norm * gains.astype(jnp.float32)[None, :]).astype(jnp.bfloat16)

def server_attention(operands):
    query_rows, fresh_key, fresh_value, cached_keys, cached_values, lengths = operands
    score_scale = 1.0 / math.sqrt(HEAD_SIZE)
    finish = jnp.cumsum(lengths)
    starts = finish - lengths
    key_rows = jnp.arange(SLOT_CAPACITY, dtype=jnp.int32)
    inside = (key_rows[None, :] >= starts[:, None]) & (key_rows[None, :] < finish[:, None])
    inside = inside[:, None, None, :]
    scores = jnp.einsum('igrd,tgd->igrt', query_rows.astype(jnp.float32), cached_keys.astype(jnp.float32)) * score_scale
    self_score = jnp.einsum('igrd,igd->igr', query_rows.astype(jnp.float32), fresh_key.astype(jnp.float32)) * score_scale
    running_max = jnp.maximum(lax.optimization_barrier(jnp.max(jnp.where(inside, scores, -jnp.inf), axis=-1)), self_score)
    exps = jnp.where(inside, jnp.exp(scores - running_max[..., None]), 0.0)
    self_exp = jnp.exp(self_score - running_max)
    running_sum = lax.optimization_barrier(jnp.sum(exps, axis=-1)) + self_exp
    numerators = exps.astype(jnp.bfloat16)
    self_numerator = self_exp.astype(jnp.bfloat16)
    combined_out = jnp.einsum('igrt,tgd->igrd', numerators.astype(jnp.float32), cached_values.astype(jnp.float32))
    combined_out = combined_out + self_numerator.astype(jnp.float32)[..., None] * fresh_value.astype(jnp.float32)[:, :, None, :]
    return (combined_out / running_sum[..., None]).astype(jnp.bfloat16)

def reference(hidden, cache_len, request_serving_order, rotated_key_cache, stored_value_cache, attn_gain, w_query, key_projection_weight, value_projection_weight, b_query, key_bias, value_bias, w_out, mlp_gain, w_gate, w_up, w_down):
    residual = hidden.astype(jnp.float32)
    inverse = jnp.argsort(request_serving_order).astype(jnp.int32)
    head_repeat_count = QUERY_HEADS // KEY_VALUE_HEADS
    for current_layer_index in range(LAYER_COUNT):
        normed = normalize(residual, attn_gain)
        query_gathered_all = jnp.dot(normed, w_query, preferred_element_type=jnp.float32) + b_query.astype(jnp.float32)[None, :]
        key_gathered_all = jnp.dot(normed, key_projection_weight, preferred_element_type=jnp.float32) + key_bias.astype(jnp.float32)[None, :]
        value_gathered_all = jnp.dot(normed, value_projection_weight, preferred_element_type=jnp.float32) + value_bias.astype(jnp.float32)[None, :]
        lengths = cache_len[current_layer_index]
        dealt_requests = jnp.take(lengths, request_serving_order)
        token_positions = dealt_requests.astype(jnp.float32)
        query_rows = apply_rotation(jnp.take(query_gathered_all, request_serving_order, axis=0).reshape(REQUEST_TOTAL, KEY_VALUE_HEADS, head_repeat_count, HEAD_SIZE), token_positions).astype(jnp.bfloat16)
        fresh_key = apply_rotation(jnp.take(key_gathered_all, request_serving_order, axis=0).reshape(REQUEST_TOTAL, KEY_VALUE_HEADS, HEAD_SIZE), token_positions).astype(jnp.bfloat16)
        fresh_value = jnp.take(value_gathered_all, request_serving_order, axis=0).reshape(REQUEST_TOTAL, KEY_VALUE_HEADS, HEAD_SIZE).astype(jnp.bfloat16)
        attention_output = lax.map(server_attention, (query_rows.reshape(N_REQ, REQUESTS_PER_IDX, KEY_VALUE_HEADS, head_repeat_count, HEAD_SIZE), fresh_key.reshape(N_REQ, REQUESTS_PER_IDX, KEY_VALUE_HEADS, HEAD_SIZE), fresh_value.reshape(N_REQ, REQUESTS_PER_IDX, KEY_VALUE_HEADS, HEAD_SIZE), rotated_key_cache[current_layer_index].reshape(N_REQ, SLOT_CAPACITY, KEY_VALUE_HEADS, HEAD_SIZE), stored_value_cache[current_layer_index].reshape(N_REQ, SLOT_CAPACITY, KEY_VALUE_HEADS, HEAD_SIZE), dealt_requests.reshape(N_REQ, REQUESTS_PER_IDX)))
        attention_output = jnp.take(attention_output.reshape(REQUEST_TOTAL, QUERY_HEADS * HEAD_SIZE), inverse, axis=0)
        residual = residual + jnp.dot(attention_output, w_out, preferred_element_type=jnp.float32)
        normed_mlp = normalize(residual, mlp_gain)
        gate_value = jnp.dot(normed_mlp, w_gate, preferred_element_type=jnp.float32)
        up_value = jnp.dot(normed_mlp, w_up, preferred_element_type=jnp.float32)
        inner = (jax.nn.silu(gate_value) * up_value).astype(jnp.bfloat16)
        residual = residual + jnp.dot(inner, w_down, preferred_element_type=jnp.float32)
    return residual
```

```python
import math

import jax
import jax.numpy as jnp
from jax import lax
from jax.sharding import PartitionSpec as P

MODEL_WIDTH = 8192
HEAD_SIZE = 128
LAYER_COUNT = 2


EPS = 1e-06
LOG_BASE = math.log(1000000.0)


def scatter_sum(block, axis):
    count = lax.axis_size(axis)
    index = lax.axis_index(axis)
    chunks = block.reshape(count, block.shape[0] // count, *block.shape[1:])
    total = jnp.take(chunks, index, axis=0)
    for shift in range(1, count):
        piece = jnp.take(chunks, (index + shift) % count, axis=0)
        total = total + lax.ppermute(
            piece, axis, [(j, (j + shift) % count) for j in range(count)]
        )
    return total


def rows_for_weights(block):
    wide = lax.all_gather(block, "kv", axis=1, tiled=True)
    return lax.all_to_all(wide, "req", 1, 0, tiled=True)


def apply_rotation(values, token_positions):
    half_width = values.shape[-1] // 2
    frequency = jnp.exp(
        -LOG_BASE * jnp.arange(half_width, dtype=jnp.float32) * 2.0 / values.shape[-1]
    )
    angles = token_positions[:, None] * frequency[None, :]
    reshape_to = (angles.shape[0],) + (1,) * (values.ndim - 2) + (half_width,)
    cosine = jnp.cos(angles).reshape(reshape_to)
    sine_part = jnp.sin(angles).reshape(reshape_to)
    front_half = values[..., :half_width]
    back_half = values[..., half_width:]
    return jnp.concatenate(
        [front_half * cosine - back_half * sine_part, back_half * cosine + front_half * sine_part],
        axis=-1,
    )


def normalize(residual, gains):
    square_sum = jnp.sum(residual * residual, axis=1)
    all_squares = lax.psum(square_sum, "kv")
    inv_norm = lax.rsqrt(all_squares / MODEL_WIDTH + EPS)
    return (residual * inv_norm[:, None] * gains.astype(jnp.float32)[None, :]).astype(jnp.bfloat16)


def attend(query_rows, fresh_key, fresh_value, cached_keys, cached_values, lengths):
    score_scale = 1.0 / math.sqrt(query_rows.shape[-1])
    finish = jnp.cumsum(lengths)
    starts = finish - lengths
    capacity = cached_keys.shape[0]
    block_size = min(512, capacity)
    block_count = capacity // block_size
    self_score = (
        jnp.einsum("igrd,igd->igr", query_rows, fresh_key, preferred_element_type=jnp.float32)
        * score_scale
    )
    start_out = fresh_value.astype(jnp.float32)[:, :, None, :] * jnp.ones(
        query_rows.shape, jnp.float32
    )

    def one_block(block_index, carried):
        running_max, running_sum, accumulated = carried
        first_row = block_index * block_size
        key_block = lax.dynamic_slice_in_dim(cached_keys, first_row, block_size, 0)
        value_block = lax.dynamic_slice_in_dim(cached_values, first_row, block_size, 0)
        scores = (
            jnp.einsum("igrd,tgd->igrt", query_rows, key_block, preferred_element_type=jnp.float32)
            * score_scale
        )
        key_rows = first_row + jnp.arange(block_size, dtype=jnp.int32)
        inside = (key_rows[None, :] >= starts[:, None]) & (key_rows[None, :] < finish[:, None])
        inside = inside[:, None, None, :]
        block_max = jnp.max(jnp.where(inside, scores, -jnp.inf), axis=-1)
        new_max = jnp.maximum(running_max, block_max)
        exps = jnp.where(inside, jnp.exp(scores - new_max[..., None]), 0.0)
        rescale = jnp.exp(running_max - new_max)
        new_sum = running_sum * rescale + jnp.sum(exps, axis=-1)
        contribution = jnp.einsum(
            "igrt,tgd->igrd",
            exps.astype(jnp.bfloat16),
            value_block,
            preferred_element_type=jnp.float32,
        )
        return (new_max, new_sum, accumulated * rescale[..., None] + contribution)

    running_max, running_sum, accumulated = lax.fori_loop(
        0, block_count, one_block, (self_score, jnp.ones_like(self_score), start_out)
    )
    return (accumulated / running_sum[..., None]).astype(jnp.bfloat16)


def body(
    hidden,
    cache_len,
    request_serving_order,
    rotated_key_cache,
    stored_value_cache,
    attn_gain,
    w_query,
    key_projection_weight,
    value_projection_weight,
    b_query,
    key_bias,
    value_bias,
    w_out,
    mlp_gain,
    w_gate,
    w_up,
    w_down,
):
    req_size = lax.axis_size("req")
    kv_size = lax.axis_size("kv")
    group_ratio = req_size // kv_size
    req_index = lax.axis_index("req")
    own_rows = hidden.shape[0]
    head_dim = HEAD_SIZE
    query_width = w_query.shape[1]
    key_width = key_projection_weight.shape[1]
    kv_heads = key_width // head_dim
    capacity = rotated_key_cache.shape[1]
    w_joint = jnp.concatenate([w_query, key_projection_weight, value_projection_weight], axis=1)
    b_joint = jnp.concatenate([b_query, key_bias, value_bias]).astype(jnp.float32)
    inverse = jnp.argsort(request_serving_order)
    my_slots = lax.dynamic_slice_in_dim(request_serving_order, req_index * own_rows, own_rows)
    residual = hidden.astype(jnp.float32)
    for current_layer_index in range(LAYER_COUNT):
        normed = normalize(residual, attn_gain)
        columns = rows_for_weights(normed)
        picked = jnp.take(columns, request_serving_order, axis=0)
        combined = (
            scatter_sum(jnp.dot(picked, w_joint, preferred_element_type=jnp.float32), "req")
            + b_joint[None, :]
        )
        lengths = jnp.take(cache_len[current_layer_index], my_slots)
        token_positions = lengths.astype(jnp.float32)
        query_rows = apply_rotation(
            combined[:, :query_width].reshape(own_rows, kv_heads, -1, head_dim), token_positions
        ).astype(jnp.bfloat16)
        fresh_key = apply_rotation(
            combined[:, query_width : query_width + key_width].reshape(
                own_rows, kv_heads, head_dim
            ),
            token_positions,
        ).astype(jnp.bfloat16)
        fresh_value = (
            combined[:, query_width + key_width :]
            .reshape(own_rows, kv_heads, head_dim)
            .astype(jnp.bfloat16)
        )
        cached_keys = rotated_key_cache[current_layer_index].reshape(capacity, kv_heads, head_dim)
        cached_values = stored_value_cache[current_layer_index].reshape(
            capacity, kv_heads, head_dim
        )
        attention_output = attend(
            query_rows, fresh_key, fresh_value, cached_keys, cached_values, lengths
        ).reshape(own_rows, query_width)
        head_rows = rows_for_weights(attention_output)
        project_picked = jnp.take(head_rows, inverse, axis=0)
        residual = residual + scatter_sum(
            jnp.dot(project_picked, w_out, preferred_element_type=jnp.float32), "req"
        )
        normed_mlp = normalize(residual, mlp_gain)
        tokens = lax.all_gather(normed_mlp, "req", axis=0, tiled=True)
        hidden_cols = w_gate.shape[1]
        gate_up = lax.psum_scatter(
            jnp.concatenate(
                [
                    jnp.dot(tokens, w_gate, preferred_element_type=jnp.float32),
                    jnp.dot(tokens, w_up, preferred_element_type=jnp.float32),
                ],
                axis=1,
            ),
            "kv",
            scatter_dimension=0,
            tiled=True,
        )
        local_hidden = (jax.nn.silu(gate_up[:, :hidden_cols]) * gate_up[:, hidden_cols:]).astype(
            jnp.bfloat16
        )
        hidden_all = lax.all_gather(local_hidden, "kv", axis=0, tiled=True)
        residual = residual + scatter_sum(
            jnp.dot(hidden_all, w_down, preferred_element_type=jnp.float32), "req"
        )
    return residual


def solution(mesh):
    return jax.shard_map(
        body,
        mesh=mesh,
        in_specs=(
            P("req", "kv"),
            P(),
            P(),
            P(None, "req", "kv"),
            P(None, "req", "kv"),
            P("kv"),
            P("req", "kv"),
            P("req", "kv"),
            P("req", "kv"),
            P("kv"),
            P("kv"),
            P("kv"),
            P("req", "kv"),
            P("kv"),
            P("kv", "req"),
            P("kv", "req"),
            P("req", "kv"),
        ),
        out_specs=P("req", "kv"),
        check_vma=False,
    )
```

```python
import math

import jax
import jax.numpy as jnp
from jax import lax
from jax.sharding import PartitionSpec as P

MODEL_WIDTH = 8192
HEAD_SIZE = 128
LAYER_COUNT = 2


EPS = 1e-06
LOG_BASE = math.log(1000000.0)


def scatter_sum(block, axis):
    count = lax.axis_size(axis)
    index = lax.axis_index(axis)
    chunks = block.reshape(count, block.shape[0] // count, *block.shape[1:])
    total = jnp.take(chunks, index, axis=0)
    for shift in range(1, count):
        piece = jnp.take(chunks, (index + shift) % count, axis=0)
        total = total + lax.ppermute(
            piece, axis, [(j, (j + shift) % count) for j in range(count)]
        )
    return total


def rows_for_weights(block):
    wide = lax.all_gather(block, "kv", axis=1, tiled=True)
    return lax.all_to_all(wide, "req", 1, 0, tiled=True)


def apply_rotation(values, token_positions):
    half_width = values.shape[-1] // 2
    frequency = jnp.exp(
        -LOG_BASE * jnp.arange(half_width, dtype=jnp.float32) * 2.0 / values.shape[-1]
    )
    angles = token_positions[:, None] * frequency[None, :]
    reshape_to = (angles.shape[0],) + (1,) * (values.ndim - 2) + (half_width,)
    cosine = jnp.cos(angles).reshape(reshape_to)
    sine_part = jnp.sin(angles).reshape(reshape_to)
    front_half = values[..., :half_width]
    back_half = values[..., half_width:]
    return jnp.concatenate(
        [front_half * cosine - back_half * sine_part, back_half * cosine + front_half * sine_part],
        axis=-1,
    )


def normalize(residual, gains):
    square_sum = jnp.sum(residual * residual, axis=1)
    count = lax.axis_size("kv")
    all_squares = square_sum
    for shift in range(1, count):
        all_squares = all_squares + lax.ppermute(
            square_sum, "kv", [(j, (j + shift) % count) for j in range(count)]
        )
    inv_norm = lax.rsqrt(all_squares / MODEL_WIDTH + EPS)
    return (residual * inv_norm[:, None] * gains.astype(jnp.float32)[None, :]).astype(jnp.bfloat16)


def attend(query_rows, fresh_key, fresh_value, cached_keys, cached_values, lengths):
    score_scale = 1.0 / math.sqrt(query_rows.shape[-1])
    finish = jnp.cumsum(lengths)
    starts = finish - lengths
    capacity = cached_keys.shape[0]
    key_rows = jnp.arange(capacity, dtype=jnp.int32)
    inside = (key_rows[None, :] >= starts[:, None]) & (key_rows[None, :] < finish[:, None])
    inside = inside[:, None, None, :]
    scores = (
        jnp.einsum("igrd,tgd->igrt", query_rows, cached_keys, preferred_element_type=jnp.float32)
        * score_scale
    )
    self_score = (
        jnp.einsum("igrd,igd->igr", query_rows, fresh_key, preferred_element_type=jnp.float32)
        * score_scale
    )
    top = jnp.maximum(jnp.max(jnp.where(inside, scores, -jnp.inf), axis=-1), self_score)
    exps = jnp.where(inside, jnp.exp(scores - top[..., None]), 0.0)
    self_exp = jnp.exp(self_score - top)
    total = jnp.sum(exps, axis=-1) + self_exp
    combined = jnp.einsum(
        "igrt,tgd->igrd",
        exps.astype(jnp.bfloat16),
        cached_values,
        preferred_element_type=jnp.float32,
    )
    combined = combined + self_exp.astype(jnp.bfloat16).astype(jnp.float32)[..., None] * (
        fresh_value.astype(jnp.float32)[:, :, None, :]
    )
    return (combined / total[..., None]).astype(jnp.bfloat16)


def body(
    hidden,
    cache_len,
    request_serving_order,
    rotated_key_cache,
    stored_value_cache,
    attn_gain,
    w_query,
    key_projection_weight,
    value_projection_weight,
    b_query,
    key_bias,
    value_bias,
    w_out,
    mlp_gain,
    w_gate,
    w_up,
    w_down,
):
    req_size = lax.axis_size("req")
    kv_size = lax.axis_size("kv")
    group_ratio = req_size // kv_size
    req_index = lax.axis_index("req")
    own_rows = hidden.shape[0]
    head_dim = HEAD_SIZE
    query_width = w_query.shape[1]
    key_width = key_projection_weight.shape[1]
    kv_heads = key_width // head_dim
    capacity = rotated_key_cache.shape[1]
    w_joint = jnp.concatenate([w_query, key_projection_weight, value_projection_weight], axis=1)
    b_joint = jnp.concatenate([b_query, key_bias, value_bias]).astype(jnp.float32)
    inverse = jnp.argsort(request_serving_order)
    my_slots = lax.dynamic_slice_in_dim(request_serving_order, req_index * own_rows, own_rows)
    residual = hidden.astype(jnp.float32)
    for current_layer_index in range(LAYER_COUNT):
        normed = normalize(residual, attn_gain)
        columns = rows_for_weights(normed)
        picked = jnp.take(columns, request_serving_order, axis=0)
        combined = (
            scatter_sum(jnp.dot(picked, w_joint, preferred_element_type=jnp.float32), "req")
            + b_joint[None, :]
        )
        lengths = jnp.take(cache_len[current_layer_index], my_slots)
        token_positions = lengths.astype(jnp.float32)
        query_rows = apply_rotation(
            combined[:, :query_width].reshape(own_rows, kv_heads, -1, head_dim), token_positions
        ).astype(jnp.bfloat16)
        fresh_key = apply_rotation(
            combined[:, query_width : query_width + key_width].reshape(
                own_rows, kv_heads, head_dim
            ),
            token_positions,
        ).astype(jnp.bfloat16)
        fresh_value = (
            combined[:, query_width + key_width :]
            .reshape(own_rows, kv_heads, head_dim)
            .astype(jnp.bfloat16)
        )
        cached_keys = rotated_key_cache[current_layer_index].reshape(capacity, kv_heads, head_dim)
        cached_values = stored_value_cache[current_layer_index].reshape(
            capacity, kv_heads, head_dim
        )
        attention_output = attend(
            query_rows, fresh_key, fresh_value, cached_keys, cached_values, lengths
        ).reshape(own_rows, query_width)
        head_rows = rows_for_weights(attention_output)
        project_picked = jnp.take(head_rows, inverse, axis=0)
        residual = residual + scatter_sum(
            jnp.dot(project_picked, w_out, preferred_element_type=jnp.float32), "req"
        )
        normed_mlp = normalize(residual, mlp_gain)
        tokens = lax.all_gather(normed_mlp, "req", axis=0, tiled=True)
        hidden_cols = w_gate.shape[1]
        gate_up = lax.psum_scatter(
            jnp.concatenate(
                [
                    jnp.dot(tokens, w_gate, preferred_element_type=jnp.float32),
                    jnp.dot(tokens, w_up, preferred_element_type=jnp.float32),
                ],
                axis=1,
            ),
            "kv",
            scatter_dimension=0,
            tiled=True,
        )
        local_hidden = (jax.nn.silu(gate_up[:, :hidden_cols]) * gate_up[:, hidden_cols:]).astype(
            jnp.bfloat16
        )
        hidden_all = lax.all_gather(local_hidden, "kv", axis=0, tiled=True)
        residual = residual + scatter_sum(
            jnp.dot(hidden_all, w_down, preferred_element_type=jnp.float32), "req"
        )
    return residual


def solution(mesh):
    return jax.shard_map(
        body,
        mesh=mesh,
        in_specs=(
            P("req", "kv"),
            P(),
            P(),
            P(None, "req", "kv"),
            P(None, "req", "kv"),
            P("kv"),
            P("req", "kv"),
            P("req", "kv"),
            P("req", "kv"),
            P("kv"),
            P("kv"),
            P("kv"),
            P("req", "kv"),
            P("kv"),
            P("kv", "req"),
            P("kv", "req"),
            P("req", "kv"),
        ),
        out_specs=P("req", "kv"),
        check_vma=False,
    )
```

```python
import math

import jax
import jax.numpy as jnp
from jax import lax
from jax.sharding import PartitionSpec as P

MODEL_WIDTH = 8192
HEAD_SIZE = 128
LAYER_COUNT = 2


EPS = 1e-06
LOG_BASE = math.log(1000000.0)


def scatter_sum(block, axis):
    count = lax.axis_size(axis)
    index = lax.axis_index(axis)
    chunks = block.reshape(count, block.shape[0] // count, *block.shape[1:])
    total = jnp.take(chunks, index, axis=0)
    for shift in range(1, count):
        piece = jnp.take(chunks, (index + shift) % count, axis=0)
        total = total + lax.ppermute(
            piece, axis, [(j, (j + shift) % count) for j in range(count)]
        )
    return total


def rows_for_weights(block):
    wide = lax.all_gather(block, "kv", axis=1, tiled=True)
    return lax.all_to_all(wide, "req", 1, 0, tiled=True)


def apply_rotation(values, token_positions):
    half_width = values.shape[-1] // 2
    frequency = jnp.exp(
        -LOG_BASE * jnp.arange(half_width, dtype=jnp.float32) * 2.0 / values.shape[-1]
    )
    angles = token_positions[:, None] * frequency[None, :]
    reshape_to = (angles.shape[0],) + (1,) * (values.ndim - 2) + (half_width,)
    cosine = jnp.cos(angles).reshape(reshape_to)
    sine_part = jnp.sin(angles).reshape(reshape_to)
    front_half = values[..., :half_width]
    back_half = values[..., half_width:]
    return jnp.concatenate(
        [front_half * cosine - back_half * sine_part, back_half * cosine + front_half * sine_part],
        axis=-1,
    )


def normalize(residual, gains):
    square_sum = jnp.sum(residual * residual, axis=1)
    count = lax.axis_size("kv")
    all_squares = square_sum
    for shift in range(1, count):
        all_squares = all_squares + lax.ppermute(
            square_sum, "kv", [(j, (j + shift) % count) for j in range(count)]
        )
    inv_norm = lax.rsqrt(all_squares / MODEL_WIDTH + EPS)
    return (residual * inv_norm[:, None] * gains.astype(jnp.float32)[None, :]).astype(jnp.bfloat16)


def attend(query_rows, fresh_key, fresh_value, key_cache, value_cache, layer, lengths):
    score_scale = 1.0 / math.sqrt(query_rows.shape[-1])
    requests, kv_heads, group, head_dim = query_rows.shape
    finish = jnp.cumsum(lengths)
    starts = finish - lengths
    capacity = key_cache.shape[1]
    key_rows = jnp.arange(capacity, dtype=jnp.int32)
    inside = (key_rows[None, :] >= starts[:, None]) & (key_rows[None, :] < finish[:, None])
    inside = jnp.broadcast_to(inside[:, None, :], (requests, group, capacity)).reshape(
        requests * group, capacity
    )
    outputs = []
    for head in range(kv_heads):
        columns = slice(head * head_dim, (head + 1) * head_dim)
        head_queries = query_rows[:, head].reshape(requests * group, head_dim)
        scores = (
            lax.dot_general(
                head_queries,
                key_cache[layer, :, columns],
                (((1,), (1,)), ((), ())),
                preferred_element_type=jnp.float32,
            )
            * score_scale
        )
        self_score = (
            jnp.einsum(
                "ird,id->ir",
                query_rows[:, head],
                fresh_key[:, head],
                preferred_element_type=jnp.float32,
            ).reshape(requests * group)
            * score_scale
        )
        top = jnp.maximum(jnp.max(jnp.where(inside, scores, -jnp.inf), axis=-1), self_score)
        exps = jnp.where(inside, jnp.exp(scores - top[:, None]), 0.0)
        self_exp = jnp.exp(self_score - top)
        total = jnp.sum(exps, axis=-1) + self_exp
        combined = jnp.dot(
            exps.astype(jnp.bfloat16),
            value_cache[layer, :, columns],
            preferred_element_type=jnp.float32,
        )
        fresh = jnp.repeat(fresh_value[:, head].astype(jnp.float32), group, axis=0)
        combined = combined + self_exp.astype(jnp.bfloat16).astype(jnp.float32)[:, None] * fresh
        outputs.append((combined / total[:, None]).astype(jnp.bfloat16).reshape(requests, group, head_dim))
    return jnp.stack(outputs, axis=1)


def body(
    hidden,
    cache_len,
    request_serving_order,
    rotated_key_cache,
    stored_value_cache,
    attn_gain,
    w_query,
    key_projection_weight,
    value_projection_weight,
    b_query,
    key_bias,
    value_bias,
    w_out,
    mlp_gain,
    w_gate,
    w_up,
    w_down,
):
    req_size = lax.axis_size("req")
    kv_size = lax.axis_size("kv")
    group_ratio = req_size // kv_size
    req_index = lax.axis_index("req")
    own_rows = hidden.shape[0]
    head_dim = HEAD_SIZE
    query_width = w_query.shape[1]
    key_width = key_projection_weight.shape[1]
    kv_heads = key_width // head_dim
    capacity = rotated_key_cache.shape[1]
    w_joint = jnp.concatenate([w_query, key_projection_weight, value_projection_weight], axis=1)
    b_joint = jnp.concatenate([b_query, key_bias, value_bias]).astype(jnp.float32)
    inverse = jnp.argsort(request_serving_order)
    my_slots = lax.dynamic_slice_in_dim(request_serving_order, req_index * own_rows, own_rows)
    residual = hidden.astype(jnp.float32)
    for current_layer_index in range(LAYER_COUNT):
        normed = normalize(residual, attn_gain)
        columns = rows_for_weights(normed)
        picked = jnp.take(columns, request_serving_order, axis=0)
        combined = (
            scatter_sum(jnp.dot(picked, w_joint, preferred_element_type=jnp.float32), "req")
            + b_joint[None, :]
        )
        lengths = jnp.take(cache_len[current_layer_index], my_slots)
        token_positions = lengths.astype(jnp.float32)
        query_rows = apply_rotation(
            combined[:, :query_width].reshape(own_rows, kv_heads, -1, head_dim), token_positions
        ).astype(jnp.bfloat16)
        fresh_key = apply_rotation(
            combined[:, query_width : query_width + key_width].reshape(
                own_rows, kv_heads, head_dim
            ),
            token_positions,
        ).astype(jnp.bfloat16)
        fresh_value = (
            combined[:, query_width + key_width :]
            .reshape(own_rows, kv_heads, head_dim)
            .astype(jnp.bfloat16)
        )
        attention_output = attend(
            query_rows,
            fresh_key,
            fresh_value,
            rotated_key_cache,
            stored_value_cache,
            current_layer_index,
            lengths,
        ).reshape(own_rows, query_width)
        head_rows = rows_for_weights(attention_output)
        project_picked = jnp.take(head_rows, inverse, axis=0)
        residual = residual + scatter_sum(
            jnp.dot(project_picked, w_out, preferred_element_type=jnp.float32), "req"
        )
        normed_mlp = normalize(residual, mlp_gain)
        tokens = lax.all_gather(normed_mlp, "req", axis=0, tiled=True)
        hidden_cols = w_gate.shape[1]
        gate_up = lax.psum_scatter(
            jnp.concatenate(
                [
                    jnp.dot(tokens, w_gate, preferred_element_type=jnp.float32),
                    jnp.dot(tokens, w_up, preferred_element_type=jnp.float32),
                ],
                axis=1,
            ),
            "kv",
            scatter_dimension=0,
            tiled=True,
        )
        local_hidden = (jax.nn.silu(gate_up[:, :hidden_cols]) * gate_up[:, hidden_cols:]).astype(
            jnp.bfloat16
        )
        hidden_all = lax.all_gather(local_hidden, "kv", axis=0, tiled=True)
        residual = residual + scatter_sum(
            jnp.dot(hidden_all, w_down, preferred_element_type=jnp.float32), "req"
        )
    return residual


def solution(mesh):
    return jax.shard_map(
        body,
        mesh=mesh,
        in_specs=(
            P("req", "kv"),
            P(),
            P(),
            P(None, "req", "kv"),
            P(None, "req", "kv"),
            P("kv"),
            P("req", "kv"),
            P("req", "kv"),
            P("req", "kv"),
            P("kv"),
            P("kv"),
            P("kv"),
            P("req", "kv"),
            P("kv"),
            P("kv", "req"),
            P("kv", "req"),
            P("req", "kv"),
        ),
        out_specs=P("req", "kv"),
        check_vma=False,
    )
```

```python
import math

import jax
import jax.numpy as jnp
from jax import lax
from jax.sharding import PartitionSpec as P

MODEL_WIDTH = 8192
HEAD_SIZE = 128
LAYER_COUNT = 2


EPS = 1e-06
LOG_BASE = math.log(1000000.0)


def scatter_sum(block, axis):
    count = lax.axis_size(axis)
    index = lax.axis_index(axis)
    chunks = block.reshape(count, block.shape[0] // count, *block.shape[1:])
    total = jnp.take(chunks, index, axis=0)
    for shift in range(1, count):
        piece = jnp.take(chunks, (index + shift) % count, axis=0)
        total = total + lax.ppermute(
            piece, axis, [(j, (j + shift) % count) for j in range(count)]
        )
    return total


def rows_for_weights(block):
    req_size = lax.axis_size("req")
    kv_size = lax.axis_size("kv")
    ratio = req_size // kv_size
    width = block.shape[1] // ratio
    source_row = lax.axis_index("req")
    source_column = lax.axis_index("kv")
    received = []
    for step in range(req_size):
        part = (source_row - step) % req_size // kv_size
        piece = lax.dynamic_slice_in_dim(block, part * width, width, 1)
        pairs = []
        for row in range(req_size):
            for column in range(kv_size):
                slot = (row - step) % req_size
                target_row = column * ratio + slot // kv_size
                pairs.append((row * kv_size + column, target_row * kv_size + slot % kv_size))
        received.append(lax.ppermute(piece, ("req", "kv"), pairs))
    base = source_row % ratio * kv_size + source_column
    stacked = jnp.roll(jnp.stack(received), base, axis=0)
    return stacked.reshape(req_size * block.shape[0], width)


def apply_rotation(values, token_positions):
    half_width = values.shape[-1] // 2
    frequency = jnp.exp(
        -LOG_BASE * jnp.arange(half_width, dtype=jnp.float32) * 2.0 / values.shape[-1]
    )
    angles = token_positions[:, None] * frequency[None, :]
    reshape_to = (angles.shape[0],) + (1,) * (values.ndim - 2) + (half_width,)
    cosine = jnp.cos(angles).reshape(reshape_to)
    sine_part = jnp.sin(angles).reshape(reshape_to)
    front_half = values[..., :half_width]
    back_half = values[..., half_width:]
    return jnp.concatenate(
        [front_half * cosine - back_half * sine_part, back_half * cosine + front_half * sine_part],
        axis=-1,
    )


def normalize(residual, gains):
    square_sum = jnp.sum(residual * residual, axis=1)
    count = lax.axis_size("kv")
    all_squares = square_sum
    for shift in range(1, count):
        all_squares = all_squares + lax.ppermute(
            square_sum, "kv", [(j, (j + shift) % count) for j in range(count)]
        )
    inv_norm = lax.rsqrt(all_squares / MODEL_WIDTH + EPS)
    return (residual * inv_norm[:, None] * gains.astype(jnp.float32)[None, :]).astype(jnp.bfloat16)


def attend(query_rows, fresh_key, fresh_value, key_cache, value_cache, layer, lengths):
    score_scale = 1.0 / math.sqrt(query_rows.shape[-1])
    requests, kv_heads, group, head_dim = query_rows.shape
    finish = jnp.cumsum(lengths)
    starts = finish - lengths
    capacity = key_cache.shape[1]
    key_rows = jnp.arange(capacity, dtype=jnp.int32)
    inside = (key_rows[None, :] >= starts[:, None]) & (key_rows[None, :] < finish[:, None])
    inside = jnp.broadcast_to(inside[:, None, :], (requests, group, capacity)).reshape(
        requests * group, capacity
    )
    outputs = []
    for head in range(kv_heads):
        columns = slice(head * head_dim, (head + 1) * head_dim)
        head_queries = query_rows[:, head].reshape(requests * group, head_dim)
        scores = (
            lax.dot_general(
                head_queries,
                key_cache[layer, :, columns],
                (((1,), (1,)), ((), ())),
                preferred_element_type=jnp.float32,
            )
            * score_scale
        )
        self_score = (
            jnp.einsum(
                "ird,id->ir",
                query_rows[:, head],
                fresh_key[:, head],
                preferred_element_type=jnp.float32,
            ).reshape(requests * group)
            * score_scale
        )
        top = jnp.maximum(jnp.max(jnp.where(inside, scores, -jnp.inf), axis=-1), self_score)
        exps = jnp.where(inside, jnp.exp(scores - top[:, None]), 0.0)
        self_exp = jnp.exp(self_score - top)
        total = jnp.sum(exps, axis=-1) + self_exp
        combined = jnp.dot(
            exps.astype(jnp.bfloat16),
            value_cache[layer, :, columns],
            preferred_element_type=jnp.float32,
        )
        fresh = jnp.repeat(fresh_value[:, head].astype(jnp.float32), group, axis=0)
        combined = combined + self_exp.astype(jnp.bfloat16).astype(jnp.float32)[:, None] * fresh
        outputs.append((combined / total[:, None]).astype(jnp.bfloat16).reshape(requests, group, head_dim))
    return jnp.stack(outputs, axis=1)


def body(
    hidden,
    cache_len,
    request_serving_order,
    rotated_key_cache,
    stored_value_cache,
    attn_gain,
    w_query,
    key_projection_weight,
    value_projection_weight,
    b_query,
    key_bias,
    value_bias,
    w_out,
    mlp_gain,
    w_gate,
    w_up,
    w_down,
):
    req_size = lax.axis_size("req")
    kv_size = lax.axis_size("kv")
    group_ratio = req_size // kv_size
    req_index = lax.axis_index("req")
    own_rows = hidden.shape[0]
    head_dim = HEAD_SIZE
    query_width = w_query.shape[1]
    key_width = key_projection_weight.shape[1]
    kv_heads = key_width // head_dim
    capacity = rotated_key_cache.shape[1]
    w_joint = jnp.concatenate([w_query, key_projection_weight, value_projection_weight], axis=1)
    b_joint = jnp.concatenate([b_query, key_bias, value_bias]).astype(jnp.float32)
    inverse = jnp.argsort(request_serving_order)
    my_slots = lax.dynamic_slice_in_dim(request_serving_order, req_index * own_rows, own_rows)
    residual = hidden.astype(jnp.float32)
    for current_layer_index in range(LAYER_COUNT):
        normed = normalize(residual, attn_gain)
        columns = rows_for_weights(normed)
        picked = jnp.take(columns, request_serving_order, axis=0)
        combined = (
            scatter_sum(jnp.dot(picked, w_joint, preferred_element_type=jnp.float32), "req")
            + b_joint[None, :]
        )
        lengths = jnp.take(cache_len[current_layer_index], my_slots)
        token_positions = lengths.astype(jnp.float32)
        query_rows = apply_rotation(
            combined[:, :query_width].reshape(own_rows, kv_heads, -1, head_dim), token_positions
        ).astype(jnp.bfloat16)
        fresh_key = apply_rotation(
            combined[:, query_width : query_width + key_width].reshape(
                own_rows, kv_heads, head_dim
            ),
            token_positions,
        ).astype(jnp.bfloat16)
        fresh_value = (
            combined[:, query_width + key_width :]
            .reshape(own_rows, kv_heads, head_dim)
            .astype(jnp.bfloat16)
        )
        attention_output = attend(
            query_rows,
            fresh_key,
            fresh_value,
            rotated_key_cache,
            stored_value_cache,
            current_layer_index,
            lengths,
        ).reshape(own_rows, query_width)
        head_rows = rows_for_weights(attention_output)
        project_picked = jnp.take(head_rows, inverse, axis=0)
        residual = residual + scatter_sum(
            jnp.dot(project_picked, w_out, preferred_element_type=jnp.float32), "req"
        )
        normed_mlp = normalize(residual, mlp_gain)
        tokens = lax.all_gather(normed_mlp, "req", axis=0, tiled=True)
        hidden_cols = w_gate.shape[1]
        gate_up = lax.psum_scatter(
            jnp.concatenate(
                [
                    jnp.dot(tokens, w_gate, preferred_element_type=jnp.float32),
                    jnp.dot(tokens, w_up, preferred_element_type=jnp.float32),
                ],
                axis=1,
            ),
            "kv",
            scatter_dimension=0,
            tiled=True,
        )
        local_hidden = (jax.nn.silu(gate_up[:, :hidden_cols]) * gate_up[:, hidden_cols:]).astype(
            jnp.bfloat16
        )
        hidden_all = lax.all_gather(local_hidden, "kv", axis=0, tiled=True)
        residual = residual + scatter_sum(
            jnp.dot(hidden_all, w_down, preferred_element_type=jnp.float32), "req"
        )
    return residual


def solution(mesh):
    return jax.shard_map(
        body,
        mesh=mesh,
        in_specs=(
            P("req", "kv"),
            P(),
            P(),
            P(None, "req", "kv"),
            P(None, "req", "kv"),
            P("kv"),
            P("req", "kv"),
            P("req", "kv"),
            P("req", "kv"),
            P("kv"),
            P("kv"),
            P("kv"),
            P("req", "kv"),
            P("kv"),
            P("kv", "req"),
            P("kv", "req"),
            P("req", "kv"),
        ),
        out_specs=P("req", "kv"),
        check_vma=False,
    )
```

```python
import math

import jax
import jax.numpy as jnp
from jax import lax
from jax.sharding import PartitionSpec as P

MODEL_WIDTH = 8192
HEAD_SIZE = 128
LAYER_COUNT = 2


EPS = 1e-06
LOG_BASE = math.log(1000000.0)


def scatter_sum(block, axis):
    count = lax.axis_size(axis)
    index = lax.axis_index(axis)
    chunks = block.reshape(count, block.shape[0] // count, *block.shape[1:])
    total = jnp.take(chunks, index, axis=0)
    for shift in range(1, count):
        piece = jnp.take(chunks, (index + shift) % count, axis=0)
        total = total + lax.ppermute(
            piece, axis, [(j, (j + shift) % count) for j in range(count)]
        )
    return total


def narrow_scatter_sum(block, axis):
    count = lax.axis_size(axis)
    index = lax.axis_index(axis)
    chunks = block.reshape(count, block.shape[0] // count, *block.shape[1:])
    total = jnp.take(chunks, index, axis=0)
    for shift in range(1, count):
        piece = jnp.take(chunks, (index + shift) % count, axis=0).astype(jnp.bfloat16)
        total = total + lax.ppermute(
            piece, axis, [(j, (j + shift) % count) for j in range(count)]
        ).astype(jnp.float32)
    return total


def rows_for_weights(block):
    wide = lax.all_gather(block, "kv", axis=1, tiled=True)
    return lax.all_to_all(wide, "req", 1, 0, tiled=True)


def apply_rotation(values, token_positions):
    half_width = values.shape[-1] // 2
    frequency = jnp.exp(
        -LOG_BASE * jnp.arange(half_width, dtype=jnp.float32) * 2.0 / values.shape[-1]
    )
    angles = token_positions[:, None] * frequency[None, :]
    reshape_to = (angles.shape[0],) + (1,) * (values.ndim - 2) + (half_width,)
    cosine = jnp.cos(angles).reshape(reshape_to)
    sine_part = jnp.sin(angles).reshape(reshape_to)
    front_half = values[..., :half_width]
    back_half = values[..., half_width:]
    return jnp.concatenate(
        [front_half * cosine - back_half * sine_part, back_half * cosine + front_half * sine_part],
        axis=-1,
    )


def normalize(residual, gains):
    square_sum = jnp.sum(residual * residual, axis=1)
    count = lax.axis_size("kv")
    all_squares = square_sum
    for shift in range(1, count):
        all_squares = all_squares + lax.ppermute(
            square_sum, "kv", [(j, (j + shift) % count) for j in range(count)]
        )
    inv_norm = lax.rsqrt(all_squares / MODEL_WIDTH + EPS)
    return (residual * inv_norm[:, None] * gains.astype(jnp.float32)[None, :]).astype(jnp.bfloat16)


def attend(query_rows, fresh_key, fresh_value, key_cache, value_cache, layer, lengths):
    score_scale = 1.0 / math.sqrt(query_rows.shape[-1])
    requests, kv_heads, group, head_dim = query_rows.shape
    finish = jnp.cumsum(lengths)
    starts = finish - lengths
    capacity = key_cache.shape[1]
    key_rows = jnp.arange(capacity, dtype=jnp.int32)
    inside = (key_rows[None, :] >= starts[:, None]) & (key_rows[None, :] < finish[:, None])
    inside = jnp.broadcast_to(inside[:, None, :], (requests, group, capacity)).reshape(
        requests * group, capacity
    )
    outputs = []
    for head in range(kv_heads):
        columns = slice(head * head_dim, (head + 1) * head_dim)
        head_queries = query_rows[:, head].reshape(requests * group, head_dim)
        scores = (
            lax.dot_general(
                head_queries,
                key_cache[layer, :, columns],
                (((1,), (1,)), ((), ())),
                preferred_element_type=jnp.float32,
            )
            * score_scale
        )
        self_score = (
            jnp.einsum(
                "ird,id->ir",
                query_rows[:, head],
                fresh_key[:, head],
                preferred_element_type=jnp.float32,
            ).reshape(requests * group)
            * score_scale
        )
        top = jnp.maximum(jnp.max(jnp.where(inside, scores, -jnp.inf), axis=-1), self_score)
        exps = jnp.where(inside, jnp.exp(scores - top[:, None]), 0.0)
        self_exp = jnp.exp(self_score - top)
        total = jnp.sum(exps, axis=-1) + self_exp
        combined = jnp.dot(
            exps.astype(jnp.bfloat16),
            value_cache[layer, :, columns],
            preferred_element_type=jnp.float32,
        )
        fresh = jnp.repeat(fresh_value[:, head].astype(jnp.float32), group, axis=0)
        combined = combined + self_exp.astype(jnp.bfloat16).astype(jnp.float32)[:, None] * fresh
        outputs.append((combined / total[:, None]).astype(jnp.bfloat16).reshape(requests, group, head_dim))
    return jnp.stack(outputs, axis=1)


def body(
    hidden,
    cache_len,
    request_serving_order,
    rotated_key_cache,
    stored_value_cache,
    attn_gain,
    w_query,
    key_projection_weight,
    value_projection_weight,
    b_query,
    key_bias,
    value_bias,
    w_out,
    mlp_gain,
    w_gate,
    w_up,
    w_down,
):
    req_size = lax.axis_size("req")
    kv_size = lax.axis_size("kv")
    group_ratio = req_size // kv_size
    req_index = lax.axis_index("req")
    own_rows = hidden.shape[0]
    head_dim = HEAD_SIZE
    query_width = w_query.shape[1]
    key_width = key_projection_weight.shape[1]
    kv_heads = key_width // head_dim
    capacity = rotated_key_cache.shape[1]
    w_joint = jnp.concatenate([w_query, key_projection_weight, value_projection_weight], axis=1)
    b_joint = jnp.concatenate([b_query, key_bias, value_bias]).astype(jnp.float32)
    inverse = jnp.argsort(request_serving_order)
    my_slots = lax.dynamic_slice_in_dim(request_serving_order, req_index * own_rows, own_rows)
    residual = hidden.astype(jnp.float32)
    for current_layer_index in range(LAYER_COUNT):
        normed = normalize(residual, attn_gain)
        columns = rows_for_weights(normed)
        picked = jnp.take(columns, request_serving_order, axis=0)
        combined = (
            scatter_sum(jnp.dot(picked, w_joint, preferred_element_type=jnp.float32), "req")
            + b_joint[None, :]
        )
        lengths = jnp.take(cache_len[current_layer_index], my_slots)
        token_positions = lengths.astype(jnp.float32)
        query_rows = apply_rotation(
            combined[:, :query_width].reshape(own_rows, kv_heads, -1, head_dim), token_positions
        ).astype(jnp.bfloat16)
        fresh_key = apply_rotation(
            combined[:, query_width : query_width + key_width].reshape(
                own_rows, kv_heads, head_dim
            ),
            token_positions,
        ).astype(jnp.bfloat16)
        fresh_value = (
            combined[:, query_width + key_width :]
            .reshape(own_rows, kv_heads, head_dim)
            .astype(jnp.bfloat16)
        )
        attention_output = attend(
            query_rows,
            fresh_key,
            fresh_value,
            rotated_key_cache,
            stored_value_cache,
            current_layer_index,
            lengths,
        ).reshape(own_rows, query_width)
        head_rows = rows_for_weights(attention_output)
        project_picked = jnp.take(head_rows, inverse, axis=0)
        residual = residual + scatter_sum(
            jnp.dot(project_picked, w_out, preferred_element_type=jnp.float32), "req"
        )
        normed_mlp = normalize(residual, mlp_gain)
        tokens = lax.all_gather(normed_mlp, "req", axis=0, tiled=True)
        hidden_cols = w_gate.shape[1]
        gate_up = narrow_scatter_sum(
            jnp.concatenate(
                [
                    jnp.dot(tokens, w_gate, preferred_element_type=jnp.float32),
                    jnp.dot(tokens, w_up, preferred_element_type=jnp.float32),
                ],
                axis=1,
            ),
            "kv",
        )
        local_hidden = (jax.nn.silu(gate_up[:, :hidden_cols]) * gate_up[:, hidden_cols:]).astype(
            jnp.bfloat16
        )
        hidden_all = lax.all_gather(local_hidden, "kv", axis=0, tiled=True)
        residual = residual + scatter_sum(
            jnp.dot(hidden_all, w_down, preferred_element_type=jnp.float32), "req"
        )
    return residual


def solution(mesh):
    return jax.shard_map(
        body,
        mesh=mesh,
        in_specs=(
            P("req", "kv"),
            P(),
            P(),
            P(None, "req", "kv"),
            P(None, "req", "kv"),
            P("kv"),
            P("req", "kv"),
            P("req", "kv"),
            P("req", "kv"),
            P("kv"),
            P("kv"),
            P("kv"),
            P("req", "kv"),
            P("kv"),
            P("kv", "req"),
            P("kv", "req"),
            P("req", "kv"),
        ),
        out_specs=P("req", "kv"),
        check_vma=False,
    )
```

```python
import math

import jax
import jax.numpy as jnp
from jax import lax
from jax.sharding import PartitionSpec as P

MODEL_WIDTH = 8192
HEAD_SIZE = 128
LAYER_COUNT = 2


EPS = 1e-06
LOG_BASE = math.log(1000000.0)


def scatter_sum(block, axis):
    count = lax.axis_size(axis)
    index = lax.axis_index(axis)
    chunks = block.reshape(count, block.shape[0] // count, *block.shape[1:])
    if count % 2 or count == 2:
        total = jnp.take(chunks, index, axis=0)
        for shift in range(1, count):
            piece = jnp.take(chunks, (index + shift) % count, axis=0)
            total = total + lax.ppermute(
                piece, axis, [(j, (j + shift) % count) for j in range(count)]
            )
        return total
    half = count // 2
    parity = index % 2
    grouped = chunks.reshape(half, 2, *chunks.shape[1:])
    mine = jnp.take(grouped, parity, axis=1)
    theirs = jnp.take(grouped, 1 - parity, axis=1)
    partial = mine + lax.ppermute(theirs, axis, [(j, j ^ 1) for j in range(count)])
    group_index = index // 2
    total = jnp.take(partial, group_index, axis=0)
    for shift in range(1, half):
        piece = jnp.take(partial, (group_index + shift) % half, axis=0)
        pairs = [
            (2 * u + p, 2 * ((u + shift) % half) + p) for u in range(half) for p in range(2)
        ]
        total = total + lax.ppermute(piece, axis, pairs)
    return total


def rows_for_weights(block):
    wide = lax.all_gather(block, "kv", axis=1, tiled=True)
    return lax.all_to_all(wide, "req", 1, 0, tiled=True)


def apply_rotation(values, token_positions):
    half_width = values.shape[-1] // 2
    frequency = jnp.exp(
        -LOG_BASE * jnp.arange(half_width, dtype=jnp.float32) * 2.0 / values.shape[-1]
    )
    angles = token_positions[:, None] * frequency[None, :]
    reshape_to = (angles.shape[0],) + (1,) * (values.ndim - 2) + (half_width,)
    cosine = jnp.cos(angles).reshape(reshape_to)
    sine_part = jnp.sin(angles).reshape(reshape_to)
    front_half = values[..., :half_width]
    back_half = values[..., half_width:]
    return jnp.concatenate(
        [front_half * cosine - back_half * sine_part, back_half * cosine + front_half * sine_part],
        axis=-1,
    )


def normalize(residual, gains):
    square_sum = jnp.sum(residual * residual, axis=1)
    count = lax.axis_size("kv")
    all_squares = square_sum
    for shift in range(1, count):
        all_squares = all_squares + lax.ppermute(
            square_sum, "kv", [(j, (j + shift) % count) for j in range(count)]
        )
    inv_norm = lax.rsqrt(all_squares / MODEL_WIDTH + EPS)
    return (residual * inv_norm[:, None] * gains.astype(jnp.float32)[None, :]).astype(jnp.bfloat16)


def attend(query_rows, fresh_key, fresh_value, key_cache, value_cache, layer, lengths):
    score_scale = 1.0 / math.sqrt(query_rows.shape[-1])
    requests, kv_heads, group, head_dim = query_rows.shape
    finish = jnp.cumsum(lengths)
    starts = finish - lengths
    capacity = key_cache.shape[1]
    key_rows = jnp.arange(capacity, dtype=jnp.int32)
    inside = (key_rows[None, :] >= starts[:, None]) & (key_rows[None, :] < finish[:, None])
    inside = jnp.broadcast_to(inside[:, None, :], (requests, group, capacity)).reshape(
        requests * group, capacity
    )
    outputs = []
    for head in range(kv_heads):
        columns = slice(head * head_dim, (head + 1) * head_dim)
        head_queries = query_rows[:, head].reshape(requests * group, head_dim)
        scores = (
            lax.dot_general(
                head_queries,
                key_cache[layer, :, columns],
                (((1,), (1,)), ((), ())),
                preferred_element_type=jnp.float32,
            )
            * score_scale
        )
        self_score = (
            jnp.einsum(
                "ird,id->ir",
                query_rows[:, head],
                fresh_key[:, head],
                preferred_element_type=jnp.float32,
            ).reshape(requests * group)
            * score_scale
        )
        top = jnp.maximum(jnp.max(jnp.where(inside, scores, -jnp.inf), axis=-1), self_score)
        exps = jnp.where(inside, jnp.exp(scores - top[:, None]), 0.0)
        self_exp = jnp.exp(self_score - top)
        total = jnp.sum(exps, axis=-1) + self_exp
        combined = jnp.dot(
            exps.astype(jnp.bfloat16),
            value_cache[layer, :, columns],
            preferred_element_type=jnp.float32,
        )
        fresh = jnp.repeat(fresh_value[:, head].astype(jnp.float32), group, axis=0)
        combined = combined + self_exp.astype(jnp.bfloat16).astype(jnp.float32)[:, None] * fresh
        outputs.append((combined / total[:, None]).astype(jnp.bfloat16).reshape(requests, group, head_dim))
    return jnp.stack(outputs, axis=1)


def body(
    hidden,
    cache_len,
    request_serving_order,
    rotated_key_cache,
    stored_value_cache,
    attn_gain,
    w_query,
    key_projection_weight,
    value_projection_weight,
    b_query,
    key_bias,
    value_bias,
    w_out,
    mlp_gain,
    w_gate,
    w_up,
    w_down,
):
    req_size = lax.axis_size("req")
    kv_size = lax.axis_size("kv")
    group_ratio = req_size // kv_size
    req_index = lax.axis_index("req")
    own_rows = hidden.shape[0]
    head_dim = HEAD_SIZE
    query_width = w_query.shape[1]
    key_width = key_projection_weight.shape[1]
    kv_heads = key_width // head_dim
    capacity = rotated_key_cache.shape[1]
    w_joint = jnp.concatenate([w_query, key_projection_weight, value_projection_weight], axis=1)
    b_joint = jnp.concatenate([b_query, key_bias, value_bias]).astype(jnp.float32)
    inverse = jnp.argsort(request_serving_order)
    my_slots = lax.dynamic_slice_in_dim(request_serving_order, req_index * own_rows, own_rows)
    residual = hidden.astype(jnp.float32)
    for current_layer_index in range(LAYER_COUNT):
        normed = normalize(residual, attn_gain)
        columns = rows_for_weights(normed)
        picked = jnp.take(columns, request_serving_order, axis=0)
        combined = (
            scatter_sum(jnp.dot(picked, w_joint, preferred_element_type=jnp.float32), "req")
            + b_joint[None, :]
        )
        lengths = jnp.take(cache_len[current_layer_index], my_slots)
        token_positions = lengths.astype(jnp.float32)
        query_rows = apply_rotation(
            combined[:, :query_width].reshape(own_rows, kv_heads, -1, head_dim), token_positions
        ).astype(jnp.bfloat16)
        fresh_key = apply_rotation(
            combined[:, query_width : query_width + key_width].reshape(
                own_rows, kv_heads, head_dim
            ),
            token_positions,
        ).astype(jnp.bfloat16)
        fresh_value = (
            combined[:, query_width + key_width :]
            .reshape(own_rows, kv_heads, head_dim)
            .astype(jnp.bfloat16)
        )
        attention_output = attend(
            query_rows,
            fresh_key,
            fresh_value,
            rotated_key_cache,
            stored_value_cache,
            current_layer_index,
            lengths,
        ).reshape(own_rows, query_width)
        head_rows = rows_for_weights(attention_output)
        project_picked = jnp.take(head_rows, inverse, axis=0)
        residual = residual + scatter_sum(
            jnp.dot(project_picked, w_out, preferred_element_type=jnp.float32), "req"
        )
        normed_mlp = normalize(residual, mlp_gain)
        tokens = lax.all_gather(normed_mlp, "req", axis=0, tiled=True)
        hidden_cols = w_gate.shape[1]
        gate_up = lax.psum_scatter(
            jnp.concatenate(
                [
                    jnp.dot(tokens, w_gate, preferred_element_type=jnp.float32),
                    jnp.dot(tokens, w_up, preferred_element_type=jnp.float32),
                ],
                axis=1,
            ),
            "kv",
            scatter_dimension=0,
            tiled=True,
        )
        local_hidden = (jax.nn.silu(gate_up[:, :hidden_cols]) * gate_up[:, hidden_cols:]).astype(
            jnp.bfloat16
        )
        hidden_all = lax.all_gather(local_hidden, "kv", axis=0, tiled=True)
        residual = residual + scatter_sum(
            jnp.dot(hidden_all, w_down, preferred_element_type=jnp.float32), "req"
        )
    return residual


def solution(mesh):
    return jax.shard_map(
        body,
        mesh=mesh,
        in_specs=(
            P("req", "kv"),
            P(),
            P(),
            P(None, "req", "kv"),
            P(None, "req", "kv"),
            P("kv"),
            P("req", "kv"),
            P("req", "kv"),
            P("req", "kv"),
            P("kv"),
            P("kv"),
            P("kv"),
            P("req", "kv"),
            P("kv"),
            P("kv", "req"),
            P("kv", "req"),
            P("req", "kv"),
        ),
        out_specs=P("req", "kv"),
        check_vma=False,
    )
```

```python
import math

import jax
import jax.numpy as jnp
from jax import lax
from jax.sharding import PartitionSpec as P

MODEL_WIDTH = 8192
HEAD_SIZE = 128
LAYER_COUNT = 2


EPS = 1e-06
LOG_BASE = math.log(1000000.0)


def scatter_sum(block, axis):
    count = lax.axis_size(axis)
    index = lax.axis_index(axis)
    chunks = block.reshape(count, block.shape[0] // count, *block.shape[1:])
    if count % 2 or count == 2:
        total = jnp.take(chunks, index, axis=0)
        for shift in range(1, count):
            piece = jnp.take(chunks, (index + shift) % count, axis=0)
            total = total + lax.ppermute(
                piece, axis, [(j, (j + shift) % count) for j in range(count)]
            )
        return total
    half = count // 2
    parity = index % 2
    grouped = chunks.reshape(half, 2, *chunks.shape[1:])
    mine = jnp.take(grouped, parity, axis=1)
    theirs = jnp.take(grouped, 1 - parity, axis=1)
    partial = mine + lax.ppermute(theirs, axis, [(j, j ^ 1) for j in range(count)])
    group_index = index // 2
    total = jnp.take(partial, group_index, axis=0)
    for shift in range(1, half):
        piece = jnp.take(partial, (group_index + shift) % half, axis=0)
        pairs = [
            (2 * u + p, 2 * ((u + shift) % half) + p) for u in range(half) for p in range(2)
        ]
        total = total + lax.ppermute(piece, axis, pairs)
    return total


def gather_by_permute(block, axis):
    count = lax.axis_size(axis)
    index = lax.axis_index(axis)
    pieces = [block]
    for shift in range(1, count):
        pieces.append(
            lax.ppermute(block, axis, [(j, (j + shift) % count) for j in range(count)])
        )
    stacked = jnp.stack(pieces[:1] + pieces[1:][::-1])
    return jnp.roll(stacked, index, axis=0)


def rows_for_weights(block):
    req_size = lax.axis_size("req")
    kv_size = lax.axis_size("kv")
    ratio = req_size // kv_size
    rows, width = block.shape[0], block.shape[1] // ratio
    wide = gather_by_permute(block, "kv").reshape(kv_size, rows, ratio, width)
    wide = wide.transpose(0, 2, 1, 3).reshape(req_size * rows, width)
    return lax.all_to_all(wide, "req", 0, 0, tiled=True)


def apply_rotation(values, token_positions):
    half_width = values.shape[-1] // 2
    frequency = jnp.exp(
        -LOG_BASE * jnp.arange(half_width, dtype=jnp.float32) * 2.0 / values.shape[-1]
    )
    angles = token_positions[:, None] * frequency[None, :]
    reshape_to = (angles.shape[0],) + (1,) * (values.ndim - 2) + (half_width,)
    cosine = jnp.cos(angles).reshape(reshape_to)
    sine_part = jnp.sin(angles).reshape(reshape_to)
    front_half = values[..., :half_width]
    back_half = values[..., half_width:]
    return jnp.concatenate(
        [front_half * cosine - back_half * sine_part, back_half * cosine + front_half * sine_part],
        axis=-1,
    )


def normalize(residual, gains):
    square_sum = jnp.sum(residual * residual, axis=1)
    count = lax.axis_size("kv")
    all_squares = square_sum
    for shift in range(1, count):
        all_squares = all_squares + lax.ppermute(
            square_sum, "kv", [(j, (j + shift) % count) for j in range(count)]
        )
    inv_norm = lax.rsqrt(all_squares / MODEL_WIDTH + EPS)
    return (residual * inv_norm[:, None] * gains.astype(jnp.float32)[None, :]).astype(jnp.bfloat16)


def attend(query_rows, fresh_key, fresh_value, key_cache, value_cache, layer, lengths):
    score_scale = 1.0 / math.sqrt(query_rows.shape[-1])
    requests, kv_heads, group, head_dim = query_rows.shape
    finish = jnp.cumsum(lengths)
    starts = finish - lengths
    capacity = key_cache.shape[1]
    key_rows = jnp.arange(capacity, dtype=jnp.int32)
    inside = (key_rows[None, :] >= starts[:, None]) & (key_rows[None, :] < finish[:, None])
    inside = jnp.broadcast_to(inside[:, None, :], (requests, group, capacity)).reshape(
        requests * group, capacity
    )
    outputs = []
    for head in range(kv_heads):
        columns = slice(head * head_dim, (head + 1) * head_dim)
        head_queries = query_rows[:, head].reshape(requests * group, head_dim)
        scores = (
            lax.dot_general(
                head_queries,
                key_cache[layer, :, columns],
                (((1,), (1,)), ((), ())),
                preferred_element_type=jnp.float32,
            )
            * score_scale
        )
        self_score = (
            jnp.einsum(
                "ird,id->ir",
                query_rows[:, head],
                fresh_key[:, head],
                preferred_element_type=jnp.float32,
            ).reshape(requests * group)
            * score_scale
        )
        top = jnp.maximum(jnp.max(jnp.where(inside, scores, -jnp.inf), axis=-1), self_score)
        exps = jnp.where(inside, jnp.exp(scores - top[:, None]), 0.0)
        self_exp = jnp.exp(self_score - top)
        total = jnp.sum(exps, axis=-1) + self_exp
        combined = jnp.dot(
            exps.astype(jnp.bfloat16),
            value_cache[layer, :, columns],
            preferred_element_type=jnp.float32,
        )
        fresh = jnp.repeat(fresh_value[:, head].astype(jnp.float32), group, axis=0)
        combined = combined + self_exp.astype(jnp.bfloat16).astype(jnp.float32)[:, None] * fresh
        outputs.append((combined / total[:, None]).astype(jnp.bfloat16).reshape(requests, group, head_dim))
    return jnp.stack(outputs, axis=1)


def body(
    hidden,
    cache_len,
    request_serving_order,
    rotated_key_cache,
    stored_value_cache,
    attn_gain,
    w_query,
    key_projection_weight,
    value_projection_weight,
    b_query,
    key_bias,
    value_bias,
    w_out,
    mlp_gain,
    w_gate,
    w_up,
    w_down,
):
    req_size = lax.axis_size("req")
    kv_size = lax.axis_size("kv")
    group_ratio = req_size // kv_size
    req_index = lax.axis_index("req")
    own_rows = hidden.shape[0]
    head_dim = HEAD_SIZE
    query_width = w_query.shape[1]
    key_width = key_projection_weight.shape[1]
    kv_heads = key_width // head_dim
    capacity = rotated_key_cache.shape[1]
    w_joint = jnp.concatenate([w_query, key_projection_weight, value_projection_weight], axis=1)
    b_joint = jnp.concatenate([b_query, key_bias, value_bias]).astype(jnp.float32)
    inverse = jnp.argsort(request_serving_order)
    my_slots = lax.dynamic_slice_in_dim(request_serving_order, req_index * own_rows, own_rows)
    residual = hidden.astype(jnp.float32)
    for current_layer_index in range(LAYER_COUNT):
        normed = normalize(residual, attn_gain)
        columns = rows_for_weights(normed)
        picked = jnp.take(columns, request_serving_order, axis=0)
        combined = (
            scatter_sum(jnp.dot(picked, w_joint, preferred_element_type=jnp.float32), "req")
            + b_joint[None, :]
        )
        lengths = jnp.take(cache_len[current_layer_index], my_slots)
        token_positions = lengths.astype(jnp.float32)
        query_rows = apply_rotation(
            combined[:, :query_width].reshape(own_rows, kv_heads, -1, head_dim), token_positions
        ).astype(jnp.bfloat16)
        fresh_key = apply_rotation(
            combined[:, query_width : query_width + key_width].reshape(
                own_rows, kv_heads, head_dim
            ),
            token_positions,
        ).astype(jnp.bfloat16)
        fresh_value = (
            combined[:, query_width + key_width :]
            .reshape(own_rows, kv_heads, head_dim)
            .astype(jnp.bfloat16)
        )
        attention_output = attend(
            query_rows,
            fresh_key,
            fresh_value,
            rotated_key_cache,
            stored_value_cache,
            current_layer_index,
            lengths,
        ).reshape(own_rows, query_width)
        head_rows = rows_for_weights(attention_output)
        project_picked = jnp.take(head_rows, inverse, axis=0)
        residual = residual + scatter_sum(
            jnp.dot(project_picked, w_out, preferred_element_type=jnp.float32), "req"
        )
        normed_mlp = normalize(residual, mlp_gain)
        tokens = lax.all_gather(normed_mlp, "req", axis=0, tiled=True)
        hidden_cols = w_gate.shape[1]
        gate_up = lax.psum_scatter(
            jnp.concatenate(
                [
                    jnp.dot(tokens, w_gate, preferred_element_type=jnp.float32),
                    jnp.dot(tokens, w_up, preferred_element_type=jnp.float32),
                ],
                axis=1,
            ),
            "kv",
            scatter_dimension=0,
            tiled=True,
        )
        local_hidden = (jax.nn.silu(gate_up[:, :hidden_cols]) * gate_up[:, hidden_cols:]).astype(
            jnp.bfloat16
        )
        hidden_all = gather_by_permute(local_hidden, "kv").reshape(-1, local_hidden.shape[1])
        residual = residual + scatter_sum(
            jnp.dot(hidden_all, w_down, preferred_element_type=jnp.float32), "req"
        )
    return residual


def solution(mesh):
    return jax.shard_map(
        body,
        mesh=mesh,
        in_specs=(
            P("req", "kv"),
            P(),
            P(),
            P(None, "req", "kv"),
            P(None, "req", "kv"),
            P("kv"),
            P("req", "kv"),
            P("req", "kv"),
            P("req", "kv"),
            P("kv"),
            P("kv"),
            P("kv"),
            P("req", "kv"),
            P("kv"),
            P("kv", "req"),
            P("kv", "req"),
            P("req", "kv"),
        ),
        out_specs=P("req", "kv"),
        check_vma=False,
    )
```

```python
import math

import jax
import jax.numpy as jnp
from jax import lax
from jax.sharding import PartitionSpec as P

MODEL_WIDTH = 8192
HEAD_SIZE = 128
LAYER_COUNT = 2


EPS = 1e-06
LOG_BASE = math.log(1000000.0)


def scatter_sum(block, axis):
    count = lax.axis_size(axis)
    index = lax.axis_index(axis)
    chunks = block.reshape(count, block.shape[0] // count, *block.shape[1:])
    if count % 2 or count == 2:
        total = jnp.take(chunks, index, axis=0)
        for shift in range(1, count):
            piece = jnp.take(chunks, (index + shift) % count, axis=0)
            total = total + lax.ppermute(
                piece, axis, [(j, (j + shift) % count) for j in range(count)]
            )
        return total
    half = count // 2
    parity = index % 2
    grouped = chunks.reshape(half, 2, *chunks.shape[1:])
    mine = jnp.take(grouped, parity, axis=1)
    theirs = jnp.take(grouped, 1 - parity, axis=1)
    partial = mine + lax.ppermute(theirs, axis, [(j, j ^ 1) for j in range(count)])
    group_index = index // 2
    total = jnp.take(partial, group_index, axis=0)
    for shift in range(1, half):
        piece = jnp.take(partial, (group_index + shift) % half, axis=0)
        pairs = [
            (2 * u + p, 2 * ((u + shift) % half) + p) for u in range(half) for p in range(2)
        ]
        total = total + lax.ppermute(piece, axis, pairs)
    return total


def gather_by_permute(block, axis):
    count = lax.axis_size(axis)
    index = lax.axis_index(axis)
    pieces = [block]
    for shift in range(1, count):
        pieces.append(
            lax.ppermute(block, axis, [(j, (j + shift) % count) for j in range(count)])
        )
    stacked = jnp.stack(pieces[:1] + pieces[1:][::-1])
    return jnp.roll(stacked, index, axis=0)


def rows_for_weights(block):
    req_size = lax.axis_size("req")
    kv_size = lax.axis_size("kv")
    ratio = req_size // kv_size
    rows, width = block.shape[0], block.shape[1] // ratio
    wide = gather_by_permute(block, "kv").reshape(kv_size, rows, ratio, width)
    wide = wide.transpose(0, 2, 1, 3).reshape(req_size * rows, width)
    return lax.all_to_all(wide, "req", 0, 0, tiled=True)


def apply_rotation(values, token_positions):
    half_width = values.shape[-1] // 2
    frequency = jnp.exp(
        -LOG_BASE * jnp.arange(half_width, dtype=jnp.float32) * 2.0 / values.shape[-1]
    )
    angles = token_positions[:, None] * frequency[None, :]
    reshape_to = (angles.shape[0],) + (1,) * (values.ndim - 2) + (half_width,)
    cosine = jnp.cos(angles).reshape(reshape_to)
    sine_part = jnp.sin(angles).reshape(reshape_to)
    front_half = values[..., :half_width]
    back_half = values[..., half_width:]
    return jnp.concatenate(
        [front_half * cosine - back_half * sine_part, back_half * cosine + front_half * sine_part],
        axis=-1,
    )


def normalize(residual, gains):
    square_sum = jnp.sum(residual * residual, axis=1)
    count = lax.axis_size("kv")
    all_squares = square_sum
    for shift in range(1, count):
        all_squares = all_squares + lax.ppermute(
            square_sum, "kv", [(j, (j + shift) % count) for j in range(count)]
        )
    inv_norm = lax.rsqrt(all_squares / MODEL_WIDTH + EPS)
    return (residual * inv_norm[:, None] * gains.astype(jnp.float32)[None, :]).astype(jnp.bfloat16)


def attend(query_rows, fresh_key, fresh_value, key_cache, value_cache, layer, lengths):
    score_scale = 1.0 / math.sqrt(query_rows.shape[-1])
    requests, kv_heads, group, head_dim = query_rows.shape
    finish = jnp.cumsum(lengths)
    starts = finish - lengths
    capacity = key_cache.shape[1]
    key_rows = jnp.arange(capacity, dtype=jnp.int32)
    inside = (key_rows[None, :] >= starts[:, None]) & (key_rows[None, :] < finish[:, None])
    inside = jnp.broadcast_to(inside[:, None, :], (requests, group, capacity)).reshape(
        requests * group, capacity
    )
    outputs = []
    for head in range(kv_heads):
        columns = slice(head * head_dim, (head + 1) * head_dim)
        head_queries = query_rows[:, head].reshape(requests * group, head_dim)
        scores = (
            lax.dot_general(
                head_queries,
                key_cache[layer, :, columns],
                (((1,), (1,)), ((), ())),
                preferred_element_type=jnp.float32,
            )
            * score_scale
        )
        self_score = (
            jnp.einsum(
                "ird,id->ir",
                query_rows[:, head],
                fresh_key[:, head],
                preferred_element_type=jnp.float32,
            ).reshape(requests * group)
            * score_scale
        )
        top = jnp.maximum(jnp.max(jnp.where(inside, scores, -jnp.inf), axis=-1), self_score)
        exps = jnp.where(inside, jnp.exp(scores - top[:, None]), 0.0)
        self_exp = jnp.exp(self_score - top)
        total = jnp.sum(exps, axis=-1) + self_exp
        combined = jnp.dot(
            exps.astype(jnp.bfloat16),
            value_cache[layer, :, columns],
            preferred_element_type=jnp.float32,
        )
        fresh = jnp.repeat(fresh_value[:, head].astype(jnp.float32), group, axis=0)
        combined = combined + self_exp.astype(jnp.bfloat16).astype(jnp.float32)[:, None] * fresh
        outputs.append((combined / total[:, None]).astype(jnp.bfloat16).reshape(requests, group, head_dim))
    return jnp.stack(outputs, axis=1)


def body(
    hidden,
    cache_len,
    request_serving_order,
    rotated_key_cache,
    stored_value_cache,
    attn_gain,
    w_query,
    key_projection_weight,
    value_projection_weight,
    b_query,
    key_bias,
    value_bias,
    w_out,
    mlp_gain,
    w_gate,
    w_up,
    w_down,
):
    req_size = lax.axis_size("req")
    kv_size = lax.axis_size("kv")
    group_ratio = req_size // kv_size
    req_index = lax.axis_index("req")
    own_rows = hidden.shape[0]
    head_dim = HEAD_SIZE
    query_width = w_query.shape[1]
    key_width = key_projection_weight.shape[1]
    kv_heads = key_width // head_dim
    capacity = rotated_key_cache.shape[1]
    b_joint = jnp.concatenate([b_query, key_bias, value_bias]).astype(jnp.float32)
    request_count = request_serving_order.shape[0]
    inverse = jnp.sum(
        jnp.where(
            request_serving_order[:, None] == jnp.arange(request_count, dtype=jnp.int32)[None, :],
            jnp.arange(request_count, dtype=jnp.int32)[:, None],
            0,
        ),
        axis=0,
    )
    my_slots = lax.dynamic_slice_in_dim(request_serving_order, req_index * own_rows, own_rows)
    residual = hidden.astype(jnp.float32)
    for current_layer_index in range(LAYER_COUNT):
        normed = normalize(residual, attn_gain)
        columns = rows_for_weights(normed)
        picked = jnp.take(columns, request_serving_order, axis=0)
        combined = (
            scatter_sum(
                jnp.concatenate(
                    [
                        jnp.dot(picked, weight, preferred_element_type=jnp.float32)
                        for weight in (w_query, key_projection_weight, value_projection_weight)
                    ],
                    axis=1,
                ),
                "req",
            )
            + b_joint[None, :]
        )
        lengths = jnp.take(cache_len[current_layer_index], my_slots)
        token_positions = lengths.astype(jnp.float32)
        query_rows = apply_rotation(
            combined[:, :query_width].reshape(own_rows, kv_heads, -1, head_dim), token_positions
        ).astype(jnp.bfloat16)
        fresh_key = apply_rotation(
            combined[:, query_width : query_width + key_width].reshape(
                own_rows, kv_heads, head_dim
            ),
            token_positions,
        ).astype(jnp.bfloat16)
        fresh_value = (
            combined[:, query_width + key_width :]
            .reshape(own_rows, kv_heads, head_dim)
            .astype(jnp.bfloat16)
        )
        attention_output = attend(
            query_rows,
            fresh_key,
            fresh_value,
            rotated_key_cache,
            stored_value_cache,
            current_layer_index,
            lengths,
        ).reshape(own_rows, query_width)
        head_rows = rows_for_weights(attention_output)
        project_picked = jnp.take(head_rows, inverse, axis=0)
        residual = residual + scatter_sum(
            jnp.dot(project_picked, w_out, preferred_element_type=jnp.float32), "req"
        )
        normed_mlp = normalize(residual, mlp_gain)
        tokens = lax.all_gather(normed_mlp, "req", axis=0, tiled=True)
        hidden_cols = w_gate.shape[1]
        gate_up = lax.psum_scatter(
            jnp.concatenate(
                [
                    jnp.dot(tokens, w_gate, preferred_element_type=jnp.float32),
                    jnp.dot(tokens, w_up, preferred_element_type=jnp.float32),
                ],
                axis=1,
            ),
            "kv",
            scatter_dimension=0,
            tiled=True,
        )
        local_hidden = (jax.nn.silu(gate_up[:, :hidden_cols]) * gate_up[:, hidden_cols:]).astype(
            jnp.bfloat16
        )
        hidden_all = gather_by_permute(local_hidden, "kv").reshape(-1, local_hidden.shape[1])
        residual = residual + scatter_sum(
            jnp.dot(hidden_all, w_down, preferred_element_type=jnp.float32), "req"
        )
    return residual


def solution(mesh):
    return jax.shard_map(
        body,
        mesh=mesh,
        in_specs=(
            P("req", "kv"),
            P(),
            P(),
            P(None, "req", "kv"),
            P(None, "req", "kv"),
            P("kv"),
            P("req", "kv"),
            P("req", "kv"),
            P("req", "kv"),
            P("kv"),
            P("kv"),
            P("kv"),
            P("req", "kv"),
            P("kv"),
            P("kv", "req"),
            P("kv", "req"),
            P("req", "kv"),
        ),
        out_specs=P("req", "kv"),
        check_vma=False,
    )
```

```python
import math

import jax
import jax.numpy as jnp
from jax import lax
from jax.sharding import PartitionSpec as P

MODEL_WIDTH = 8192
HEAD_SIZE = 128
LAYER_COUNT = 2


EPS = 1e-06
LOG_BASE = math.log(1000000.0)


def scatter_sum(block, axis):
    count = lax.axis_size(axis)
    index = lax.axis_index(axis)
    chunks = block.reshape(count, block.shape[0] // count, *block.shape[1:])
    if count % 2 or count == 2:
        total = jnp.take(chunks, index, axis=0)
        for shift in range(1, count):
            piece = jnp.take(chunks, (index + shift) % count, axis=0)
            total = total + lax.ppermute(
                piece, axis, [(j, (j + shift) % count) for j in range(count)]
            )
        return total
    half = count // 2
    parity = index % 2
    grouped = chunks.reshape(half, 2, *chunks.shape[1:])
    mine = jnp.take(grouped, parity, axis=1)
    theirs = jnp.take(grouped, 1 - parity, axis=1)
    partial = mine + lax.ppermute(theirs, axis, [(j, j ^ 1) for j in range(count)])
    group_index = index // 2
    total = jnp.take(partial, group_index, axis=0)
    for shift in range(1, half):
        piece = jnp.take(partial, (group_index + shift) % half, axis=0)
        pairs = [
            (2 * u + p, 2 * ((u + shift) % half) + p) for u in range(half) for p in range(2)
        ]
        total = total + lax.ppermute(piece, axis, pairs)
    return total


def gather_by_permute(block, axis):
    count = lax.axis_size(axis)
    index = lax.axis_index(axis)
    pieces = [block]
    for shift in range(1, count):
        pieces.append(
            lax.ppermute(block, axis, [(j, (j + shift) % count) for j in range(count)])
        )
    stacked = jnp.stack(pieces[:1] + pieces[1:][::-1])
    return jnp.roll(stacked, index, axis=0)


def rows_for_weights(block):
    req_size = lax.axis_size("req")
    kv_size = lax.axis_size("kv")
    ratio = req_size // kv_size
    rows, width = block.shape[0], block.shape[1] // ratio
    wide = gather_by_permute(block, "kv").reshape(kv_size, rows, ratio, width)
    wide = wide.transpose(0, 2, 1, 3).reshape(req_size * rows, width)
    return lax.all_to_all(wide, "req", 0, 0, tiled=True)


def apply_rotation(values, token_positions):
    half_width = values.shape[-1] // 2
    frequency = jnp.exp(
        -LOG_BASE * jnp.arange(half_width, dtype=jnp.float32) * 2.0 / values.shape[-1]
    )
    angles = token_positions[:, None] * frequency[None, :]
    reshape_to = (angles.shape[0],) + (1,) * (values.ndim - 2) + (half_width,)
    cosine = jnp.cos(angles).reshape(reshape_to)
    sine_part = jnp.sin(angles).reshape(reshape_to)
    front_half = values[..., :half_width]
    back_half = values[..., half_width:]
    return jnp.concatenate(
        [front_half * cosine - back_half * sine_part, back_half * cosine + front_half * sine_part],
        axis=-1,
    )


def normalize(residual, gains):
    square_sum = jnp.sum(residual * residual, axis=1)
    count = lax.axis_size("kv")
    all_squares = square_sum
    for shift in range(1, count):
        all_squares = all_squares + lax.ppermute(
            square_sum, "kv", [(j, (j + shift) % count) for j in range(count)]
        )
    inv_norm = lax.rsqrt(all_squares / MODEL_WIDTH + EPS)
    return (residual * inv_norm[:, None] * gains.astype(jnp.float32)[None, :]).astype(jnp.bfloat16)


def attend(query_rows, fresh_key, fresh_value, key_cache, value_cache, layer, lengths):
    score_scale = 1.0 / math.sqrt(query_rows.shape[-1])
    requests, kv_heads, group, head_dim = query_rows.shape
    finish = jnp.cumsum(lengths)
    starts = finish - lengths
    capacity = key_cache.shape[1]
    key_rows = jnp.arange(capacity, dtype=jnp.int32)
    inside = (key_rows[None, :] >= starts[:, None]) & (key_rows[None, :] < finish[:, None])
    inside = jnp.broadcast_to(inside[:, None, :], (requests, group, capacity)).reshape(
        requests * group, capacity
    )
    outputs = []
    for head in range(kv_heads):
        columns = slice(head * head_dim, (head + 1) * head_dim)
        head_queries = query_rows[:, head].reshape(requests * group, head_dim)
        scores = (
            lax.dot_general(
                head_queries,
                key_cache[layer, :, columns],
                (((1,), (1,)), ((), ())),
                preferred_element_type=jnp.float32,
            )
            * score_scale
        )
        self_score = (
            jnp.einsum(
                "ird,id->ir",
                query_rows[:, head],
                fresh_key[:, head],
                preferred_element_type=jnp.float32,
            ).reshape(requests * group)
            * score_scale
        )
        top = jnp.maximum(jnp.max(jnp.where(inside, scores, -jnp.inf), axis=-1), self_score)
        exps = jnp.where(inside, jnp.exp(scores - top[:, None]), 0.0)
        self_exp = jnp.exp(self_score - top)
        total = jnp.sum(exps, axis=-1) + self_exp
        combined = jnp.dot(
            exps.astype(jnp.bfloat16),
            value_cache[layer, :, columns],
            preferred_element_type=jnp.float32,
        )
        fresh = jnp.repeat(fresh_value[:, head].astype(jnp.float32), group, axis=0)
        combined = combined + self_exp.astype(jnp.bfloat16).astype(jnp.float32)[:, None] * fresh
        outputs.append((combined / total[:, None]).astype(jnp.bfloat16).reshape(requests, group, head_dim))
    return jnp.stack(outputs, axis=1)


def body(
    hidden,
    cache_len,
    request_serving_order,
    rotated_key_cache,
    stored_value_cache,
    attn_gain,
    w_query,
    key_projection_weight,
    value_projection_weight,
    b_query,
    key_bias,
    value_bias,
    w_out,
    mlp_gain,
    w_gate,
    w_up,
    w_down,
):
    req_size = lax.axis_size("req")
    kv_size = lax.axis_size("kv")
    group_ratio = req_size // kv_size
    req_index = lax.axis_index("req")
    own_rows = hidden.shape[0]
    head_dim = HEAD_SIZE
    query_width = w_query.shape[1]
    key_width = key_projection_weight.shape[1]
    kv_heads = key_width // head_dim
    capacity = rotated_key_cache.shape[1]
    b_joint = jnp.concatenate([b_query, key_bias, value_bias]).astype(jnp.float32)
    request_count = request_serving_order.shape[0]
    inverse = jnp.sum(
        jnp.where(
            request_serving_order[:, None] == jnp.arange(request_count, dtype=jnp.int32)[None, :],
            jnp.arange(request_count, dtype=jnp.int32)[:, None],
            0,
        ),
        axis=0,
    )
    my_slots = lax.dynamic_slice_in_dim(request_serving_order, req_index * own_rows, own_rows)
    residual = hidden.astype(jnp.float32)
    for current_layer_index in range(LAYER_COUNT):
        normed = normalize(residual, attn_gain)
        columns = rows_for_weights(normed)
        picked = jnp.take(columns, request_serving_order, axis=0)
        combined = (
            scatter_sum(
                jnp.concatenate(
                    [
                        jnp.dot(picked, weight, preferred_element_type=jnp.float32)
                        for weight in (w_query, key_projection_weight, value_projection_weight)
                    ],
                    axis=1,
                ),
                "req",
            )
            + b_joint[None, :]
        )
        lengths = jnp.take(cache_len[current_layer_index], my_slots)
        token_positions = lengths.astype(jnp.float32)
        query_rows = apply_rotation(
            combined[:, :query_width].reshape(own_rows, kv_heads, -1, head_dim), token_positions
        ).astype(jnp.bfloat16)
        fresh_key = apply_rotation(
            combined[:, query_width : query_width + key_width].reshape(
                own_rows, kv_heads, head_dim
            ),
            token_positions,
        ).astype(jnp.bfloat16)
        fresh_value = (
            combined[:, query_width + key_width :]
            .reshape(own_rows, kv_heads, head_dim)
            .astype(jnp.bfloat16)
        )
        attention_output = attend(
            query_rows,
            fresh_key,
            fresh_value,
            rotated_key_cache,
            stored_value_cache,
            current_layer_index,
            lengths,
        ).reshape(own_rows, query_width)
        head_rows = rows_for_weights(attention_output)
        project_picked = jnp.take(head_rows, inverse, axis=0)
        residual = residual + scatter_sum(
            jnp.dot(project_picked, w_out, preferred_element_type=jnp.float32), "req"
        )
        normed_mlp = normalize(residual, mlp_gain)
        tokens = lax.all_gather(normed_mlp, "req", axis=0, tiled=True)
        hidden_cols = w_gate.shape[1]
        split = hidden_cols // 2 // 128 * 128
        down_sum = None
        for first, last in ((0, split), (split, hidden_cols)):
            width = last - first
            gate_up = lax.psum_scatter(
                jnp.concatenate(
                    [
                        jnp.dot(tokens, w_gate[:, first:last], preferred_element_type=jnp.float32),
                        jnp.dot(tokens, w_up[:, first:last], preferred_element_type=jnp.float32),
                    ],
                    axis=1,
                ),
                "kv",
                scatter_dimension=0,
                tiled=True,
            )
            local_hidden = (jax.nn.silu(gate_up[:, :width]) * gate_up[:, width:]).astype(
                jnp.bfloat16
            )
            hidden_all = gather_by_permute(local_hidden, "kv").reshape(-1, width)
            part = jnp.dot(hidden_all, w_down[first:last], preferred_element_type=jnp.float32)
            down_sum = part if down_sum is None else down_sum + part
        residual = residual + scatter_sum(down_sum, "req")
    return residual


def solution(mesh):
    return jax.shard_map(
        body,
        mesh=mesh,
        in_specs=(
            P("req", "kv"),
            P(),
            P(),
            P(None, "req", "kv"),
            P(None, "req", "kv"),
            P("kv"),
            P("req", "kv"),
            P("req", "kv"),
            P("req", "kv"),
            P("kv"),
            P("kv"),
            P("kv"),
            P("req", "kv"),
            P("kv"),
            P("kv", "req"),
            P("kv", "req"),
            P("req", "kv"),
        ),
        out_specs=P("req", "kv"),
        check_vma=False,
    )
```

```python
import math

import jax
import jax.numpy as jnp
from jax import lax
from jax.sharding import PartitionSpec as P

MODEL_WIDTH = 8192
HEAD_SIZE = 128
LAYER_COUNT = 2


EPS = 1e-06
LOG_BASE = math.log(1000000.0)


def scatter_sum(block, axis):
    count = lax.axis_size(axis)
    index = lax.axis_index(axis)
    chunks = block.reshape(count, block.shape[0] // count, *block.shape[1:])
    if count % 2 or count == 2:
        total = jnp.take(chunks, index, axis=0)
        for shift in range(1, count):
            piece = jnp.take(chunks, (index + shift) % count, axis=0)
            total = total + lax.ppermute(
                piece, axis, [(j, (j + shift) % count) for j in range(count)]
            )
        return total
    half = count // 2
    parity = index % 2
    grouped = chunks.reshape(half, 2, *chunks.shape[1:])
    mine = jnp.take(grouped, parity, axis=1)
    theirs = jnp.take(grouped, 1 - parity, axis=1)
    partial = mine + lax.ppermute(theirs, axis, [(j, j ^ 1) for j in range(count)])
    group_index = index // 2
    total = jnp.take(partial, group_index, axis=0)
    for shift in range(1, half):
        piece = jnp.take(partial, (group_index + shift) % half, axis=0)
        pairs = [
            (2 * u + p, 2 * ((u + shift) % half) + p) for u in range(half) for p in range(2)
        ]
        total = total + lax.ppermute(piece, axis, pairs)
    return total


def gather_by_permute(block, axis):
    count = lax.axis_size(axis)
    index = lax.axis_index(axis)
    pieces = [block]
    for shift in range(1, count):
        pieces.append(
            lax.ppermute(block, axis, [(j, (j + shift) % count) for j in range(count)])
        )
    stacked = jnp.stack(pieces[:1] + pieces[1:][::-1])
    return jnp.roll(stacked, index, axis=0)


def normed_rows_for_weights(residual, full_gain):
    req_size = lax.axis_size("req")
    kv_size = lax.axis_size("kv")
    rows = residual.shape[0]
    wide = gather_by_permute(residual, "kv").transpose(1, 0, 2).reshape(rows, -1)
    square_sum = jnp.sum(wide * wide, axis=1)
    inv_norm = lax.rsqrt(square_sum / MODEL_WIDTH + EPS)
    normed = (wide * inv_norm[:, None] * full_gain.astype(jnp.float32)[None, :]).astype(
        jnp.bfloat16
    )
    return lax.all_to_all(normed, "req", 1, 0, tiled=True)


def rows_for_weights(block):
    req_size = lax.axis_size("req")
    kv_size = lax.axis_size("kv")
    ratio = req_size // kv_size
    rows, width = block.shape[0], block.shape[1] // ratio
    wide = gather_by_permute(block, "kv").reshape(kv_size, rows, ratio, width)
    wide = wide.transpose(0, 2, 1, 3).reshape(req_size * rows, width)
    return lax.all_to_all(wide, "req", 0, 0, tiled=True)


def apply_rotation(values, token_positions):
    half_width = values.shape[-1] // 2
    frequency = jnp.exp(
        -LOG_BASE * jnp.arange(half_width, dtype=jnp.float32) * 2.0 / values.shape[-1]
    )
    angles = token_positions[:, None] * frequency[None, :]
    reshape_to = (angles.shape[0],) + (1,) * (values.ndim - 2) + (half_width,)
    cosine = jnp.cos(angles).reshape(reshape_to)
    sine_part = jnp.sin(angles).reshape(reshape_to)
    front_half = values[..., :half_width]
    back_half = values[..., half_width:]
    return jnp.concatenate(
        [front_half * cosine - back_half * sine_part, back_half * cosine + front_half * sine_part],
        axis=-1,
    )


def normalize(residual, gains):
    square_sum = jnp.sum(residual * residual, axis=1)
    count = lax.axis_size("kv")
    all_squares = square_sum
    for shift in range(1, count):
        all_squares = all_squares + lax.ppermute(
            square_sum, "kv", [(j, (j + shift) % count) for j in range(count)]
        )
    inv_norm = lax.rsqrt(all_squares / MODEL_WIDTH + EPS)
    return (residual * inv_norm[:, None] * gains.astype(jnp.float32)[None, :]).astype(jnp.bfloat16)


def attend(query_rows, fresh_key, fresh_value, key_cache, value_cache, layer, lengths):
    score_scale = 1.0 / math.sqrt(query_rows.shape[-1])
    requests, kv_heads, group, head_dim = query_rows.shape
    finish = jnp.cumsum(lengths)
    starts = finish - lengths
    capacity = key_cache.shape[1]
    key_rows = jnp.arange(capacity, dtype=jnp.int32)
    inside = (key_rows[None, :] >= starts[:, None]) & (key_rows[None, :] < finish[:, None])
    inside = jnp.broadcast_to(inside[:, None, :], (requests, group, capacity)).reshape(
        requests * group, capacity
    )
    outputs = []
    for head in range(kv_heads):
        columns = slice(head * head_dim, (head + 1) * head_dim)
        head_queries = query_rows[:, head].reshape(requests * group, head_dim)
        scores = (
            lax.dot_general(
                head_queries,
                key_cache[layer, :, columns],
                (((1,), (1,)), ((), ())),
                preferred_element_type=jnp.float32,
            )
            * score_scale
        )
        self_score = (
            jnp.einsum(
                "ird,id->ir",
                query_rows[:, head],
                fresh_key[:, head],
                preferred_element_type=jnp.float32,
            ).reshape(requests * group)
            * score_scale
        )
        top = jnp.maximum(jnp.max(jnp.where(inside, scores, -jnp.inf), axis=-1), self_score)
        exps = jnp.where(inside, jnp.exp(scores - top[:, None]), 0.0)
        self_exp = jnp.exp(self_score - top)
        total = jnp.sum(exps, axis=-1) + self_exp
        combined = jnp.dot(
            exps.astype(jnp.bfloat16),
            value_cache[layer, :, columns],
            preferred_element_type=jnp.float32,
        )
        fresh = jnp.repeat(fresh_value[:, head].astype(jnp.float32), group, axis=0)
        combined = combined + self_exp.astype(jnp.bfloat16).astype(jnp.float32)[:, None] * fresh
        outputs.append((combined / total[:, None]).astype(jnp.bfloat16).reshape(requests, group, head_dim))
    return jnp.stack(outputs, axis=1)


def body(
    hidden,
    cache_len,
    request_serving_order,
    rotated_key_cache,
    stored_value_cache,
    attn_gain,
    w_query,
    key_projection_weight,
    value_projection_weight,
    b_query,
    key_bias,
    value_bias,
    w_out,
    mlp_gain,
    w_gate,
    w_up,
    w_down,
):
    req_size = lax.axis_size("req")
    kv_size = lax.axis_size("kv")
    group_ratio = req_size // kv_size
    req_index = lax.axis_index("req")
    own_rows = hidden.shape[0]
    head_dim = HEAD_SIZE
    query_width = w_query.shape[1]
    key_width = key_projection_weight.shape[1]
    kv_heads = key_width // head_dim
    capacity = rotated_key_cache.shape[1]
    b_joint = jnp.concatenate([b_query, key_bias, value_bias]).astype(jnp.float32)
    request_count = request_serving_order.shape[0]
    inverse = jnp.sum(
        jnp.where(
            request_serving_order[:, None] == jnp.arange(request_count, dtype=jnp.int32)[None, :],
            jnp.arange(request_count, dtype=jnp.int32)[:, None],
            0,
        ),
        axis=0,
    )
    my_slots = lax.dynamic_slice_in_dim(request_serving_order, req_index * own_rows, own_rows)
    residual = hidden.astype(jnp.float32)
    full_attn_gain = lax.all_gather(attn_gain, "kv", axis=0, tiled=True)
    for current_layer_index in range(LAYER_COUNT):
        columns = normed_rows_for_weights(residual, full_attn_gain)
        picked = jnp.take(columns, request_serving_order, axis=0)
        combined = (
            scatter_sum(
                jnp.concatenate(
                    [
                        jnp.dot(picked, weight, preferred_element_type=jnp.float32)
                        for weight in (w_query, key_projection_weight, value_projection_weight)
                    ],
                    axis=1,
                ),
                "req",
            )
            + b_joint[None, :]
        )
        lengths = jnp.take(cache_len[current_layer_index], my_slots)
        token_positions = lengths.astype(jnp.float32)
        query_rows = apply_rotation(
            combined[:, :query_width].reshape(own_rows, kv_heads, -1, head_dim), token_positions
        ).astype(jnp.bfloat16)
        fresh_key = apply_rotation(
            combined[:, query_width : query_width + key_width].reshape(
                own_rows, kv_heads, head_dim
            ),
            token_positions,
        ).astype(jnp.bfloat16)
        fresh_value = (
            combined[:, query_width + key_width :]
            .reshape(own_rows, kv_heads, head_dim)
            .astype(jnp.bfloat16)
        )
        attention_output = attend(
            query_rows,
            fresh_key,
            fresh_value,
            rotated_key_cache,
            stored_value_cache,
            current_layer_index,
            lengths,
        ).reshape(own_rows, query_width)
        head_rows = rows_for_weights(attention_output)
        project_picked = jnp.take(head_rows, inverse, axis=0)
        residual = residual + scatter_sum(
            jnp.dot(project_picked, w_out, preferred_element_type=jnp.float32), "req"
        )
        normed_mlp = normalize(residual, mlp_gain)
        tokens = lax.all_gather(normed_mlp, "req", axis=0, tiled=True)
        hidden_cols = w_gate.shape[1]
        gate_up = lax.psum_scatter(
            jnp.concatenate(
                [
                    jnp.dot(tokens, w_gate, preferred_element_type=jnp.float32),
                    jnp.dot(tokens, w_up, preferred_element_type=jnp.float32),
                ],
                axis=1,
            ),
            "kv",
            scatter_dimension=0,
            tiled=True,
        )
        local_hidden = (jax.nn.silu(gate_up[:, :hidden_cols]) * gate_up[:, hidden_cols:]).astype(
            jnp.bfloat16
        )
        hidden_all = gather_by_permute(local_hidden, "kv").reshape(-1, local_hidden.shape[1])
        residual = residual + scatter_sum(
            jnp.dot(hidden_all, w_down, preferred_element_type=jnp.float32), "req"
        )
    return residual


def solution(mesh):
    return jax.shard_map(
        body,
        mesh=mesh,
        in_specs=(
            P("req", "kv"),
            P(),
            P(),
            P(None, "req", "kv"),
            P(None, "req", "kv"),
            P("kv"),
            P("req", "kv"),
            P("req", "kv"),
            P("req", "kv"),
            P("kv"),
            P("kv"),
            P("kv"),
            P("req", "kv"),
            P("kv"),
            P("kv", "req"),
            P("kv", "req"),
            P("req", "kv"),
        ),
        out_specs=P("req", "kv"),
        check_vma=False,
    )
```

```python
import math

import jax
import jax.numpy as jnp
from jax import lax
from jax.experimental.layout import Layout, with_layout_constraint
from jax.sharding import PartitionSpec as P

MODEL_WIDTH = 8192
HEAD_SIZE = 128
LAYER_COUNT = 2


EPS = 1e-06
LOG_BASE = math.log(1000000.0)


def scatter_sum(block, axis):
    count = lax.axis_size(axis)
    index = lax.axis_index(axis)
    chunks = block.reshape(count, block.shape[0] // count, *block.shape[1:])
    if count % 2 or count == 2:
        total = jnp.take(chunks, index, axis=0)
        for shift in range(1, count):
            piece = jnp.take(chunks, (index + shift) % count, axis=0)
            total = total + lax.ppermute(
                piece, axis, [(j, (j + shift) % count) for j in range(count)]
            )
        return total
    half = count // 2
    parity = index % 2
    grouped = chunks.reshape(half, 2, *chunks.shape[1:])
    mine = jnp.take(grouped, parity, axis=1)
    theirs = jnp.take(grouped, 1 - parity, axis=1)
    partial = mine + lax.ppermute(theirs, axis, [(j, j ^ 1) for j in range(count)])
    group_index = index // 2
    total = jnp.take(partial, group_index, axis=0)
    for shift in range(1, half):
        piece = jnp.take(partial, (group_index + shift) % half, axis=0)
        pairs = [
            (2 * u + p, 2 * ((u + shift) % half) + p) for u in range(half) for p in range(2)
        ]
        total = total + lax.ppermute(piece, axis, pairs)
    return total


def gather_by_permute(block, axis):
    count = lax.axis_size(axis)
    index = lax.axis_index(axis)
    pieces = [block]
    for shift in range(1, count):
        pieces.append(
            lax.ppermute(block, axis, [(j, (j + shift) % count) for j in range(count)])
        )
    stacked = jnp.stack(pieces[:1] + pieces[1:][::-1])
    return jnp.roll(stacked, index, axis=0)


def rows_for_weights(block):
    req_size = lax.axis_size("req")
    kv_size = lax.axis_size("kv")
    ratio = req_size // kv_size
    rows, width = block.shape[0], block.shape[1] // ratio
    wide = gather_by_permute(block, "kv").reshape(kv_size, rows, ratio, width)
    wide = wide.transpose(0, 2, 1, 3).reshape(req_size * rows, width)
    return lax.all_to_all(wide, "req", 0, 0, tiled=True)


def apply_rotation(values, token_positions):
    half_width = values.shape[-1] // 2
    frequency = jnp.exp(
        -LOG_BASE * jnp.arange(half_width, dtype=jnp.float32) * 2.0 / values.shape[-1]
    )
    angles = token_positions[:, None] * frequency[None, :]
    reshape_to = (angles.shape[0],) + (1,) * (values.ndim - 2) + (half_width,)
    cosine = jnp.cos(angles).reshape(reshape_to)
    sine_part = jnp.sin(angles).reshape(reshape_to)
    front_half = values[..., :half_width]
    back_half = values[..., half_width:]
    return jnp.concatenate(
        [front_half * cosine - back_half * sine_part, back_half * cosine + front_half * sine_part],
        axis=-1,
    )


def normalize(residual, gains):
    square_sum = jnp.sum(residual * residual, axis=1)
    count = lax.axis_size("kv")
    all_squares = square_sum
    for shift in range(1, count):
        all_squares = all_squares + lax.ppermute(
            square_sum, "kv", [(j, (j + shift) % count) for j in range(count)]
        )
    inv_norm = lax.rsqrt(all_squares / MODEL_WIDTH + EPS)
    return (residual * inv_norm[:, None] * gains.astype(jnp.float32)[None, :]).astype(jnp.bfloat16)


def attend(query_rows, fresh_key, fresh_value, key_cache, value_cache, layer, lengths):
    score_scale = 1.0 / math.sqrt(query_rows.shape[-1])
    requests, kv_heads, group, head_dim = query_rows.shape
    finish = jnp.cumsum(lengths)
    starts = finish - lengths
    capacity = key_cache.shape[1]
    key_rows = jnp.arange(capacity, dtype=jnp.int32)
    inside = (key_rows[None, :] >= starts[:, None]) & (key_rows[None, :] < finish[:, None])
    inside = jnp.broadcast_to(inside[:, None, :], (requests, group, capacity)).reshape(
        requests * group, capacity
    )
    outputs = []
    for head in range(kv_heads):
        columns = slice(head * head_dim, (head + 1) * head_dim)
        head_queries = query_rows[:, head].reshape(requests * group, head_dim)
        scores = (
            lax.dot_general(
                head_queries,
                key_cache[layer, :, columns],
                (((1,), (1,)), ((), ())),
                preferred_element_type=jnp.float32,
            )
            * score_scale
        )
        self_score = (
            jnp.einsum(
                "ird,id->ir",
                query_rows[:, head],
                fresh_key[:, head],
                preferred_element_type=jnp.float32,
            ).reshape(requests * group)
            * score_scale
        )
        top = jnp.maximum(jnp.max(jnp.where(inside, scores, -jnp.inf), axis=-1), self_score)
        exps = jnp.where(inside, jnp.exp(scores - top[:, None]), 0.0)
        self_exp = jnp.exp(self_score - top)
        total = jnp.sum(exps, axis=-1) + self_exp
        combined = jnp.dot(
            exps.astype(jnp.bfloat16),
            value_cache[layer, :, columns],
            preferred_element_type=jnp.float32,
        )
        fresh = jnp.repeat(fresh_value[:, head].astype(jnp.float32), group, axis=0)
        combined = combined + self_exp.astype(jnp.bfloat16).astype(jnp.float32)[:, None] * fresh
        outputs.append((combined / total[:, None]).astype(jnp.bfloat16).reshape(requests, group, head_dim))
    return jnp.stack(outputs, axis=1)


def body(
    hidden,
    cache_len,
    request_serving_order,
    rotated_key_cache,
    stored_value_cache,
    attn_gain,
    w_query,
    key_projection_weight,
    value_projection_weight,
    b_query,
    key_bias,
    value_bias,
    w_out,
    mlp_gain,
    w_gate,
    w_up,
    w_down,
):
    req_size = lax.axis_size("req")
    kv_size = lax.axis_size("kv")
    group_ratio = req_size // kv_size
    req_index = lax.axis_index("req")
    own_rows = hidden.shape[0]
    head_dim = HEAD_SIZE
    query_width = w_query.shape[1]
    key_width = key_projection_weight.shape[1]
    kv_heads = key_width // head_dim
    capacity = rotated_key_cache.shape[1]
    b_joint = jnp.concatenate([b_query, key_bias, value_bias]).astype(jnp.float32)
    request_count = request_serving_order.shape[0]
    inverse = jnp.sum(
        jnp.where(
            request_serving_order[:, None] == jnp.arange(request_count, dtype=jnp.int32)[None, :],
            jnp.arange(request_count, dtype=jnp.int32)[:, None],
            0,
        ),
        axis=0,
    )
    my_slots = lax.dynamic_slice_in_dim(request_serving_order, req_index * own_rows, own_rows)
    residual = hidden.astype(jnp.float32)
    for current_layer_index in range(LAYER_COUNT):
        normed = normalize(residual, attn_gain)
        columns = rows_for_weights(normed)
        picked = jnp.take(columns, request_serving_order, axis=0)
        combined = (
            scatter_sum(
                jnp.concatenate(
                    [
                        jnp.dot(picked, weight, preferred_element_type=jnp.float32)
                        for weight in (w_query, key_projection_weight, value_projection_weight)
                    ],
                    axis=1,
                ),
                "req",
            )
            + b_joint[None, :]
        )
        lengths = jnp.take(cache_len[current_layer_index], my_slots)
        token_positions = lengths.astype(jnp.float32)
        query_rows = apply_rotation(
            combined[:, :query_width].reshape(own_rows, kv_heads, -1, head_dim), token_positions
        ).astype(jnp.bfloat16)
        fresh_key = apply_rotation(
            combined[:, query_width : query_width + key_width].reshape(
                own_rows, kv_heads, head_dim
            ),
            token_positions,
        ).astype(jnp.bfloat16)
        fresh_value = (
            combined[:, query_width + key_width :]
            .reshape(own_rows, kv_heads, head_dim)
            .astype(jnp.bfloat16)
        )
        attention_output = attend(
            query_rows,
            fresh_key,
            fresh_value,
            rotated_key_cache,
            stored_value_cache,
            current_layer_index,
            lengths,
        ).reshape(own_rows, query_width)
        head_rows = rows_for_weights(attention_output)
        project_picked = jnp.take(head_rows, inverse, axis=0)
        residual = residual + scatter_sum(
            jnp.dot(project_picked, w_out, preferred_element_type=jnp.float32), "req"
        )
        normed_mlp = normalize(residual, mlp_gain)
        tokens = lax.all_gather(normed_mlp, "req", axis=0, tiled=True)
        hidden_cols = w_gate.shape[1]
        gate_up = lax.psum_scatter(
            jnp.concatenate(
                [
                    with_layout_constraint(
                        jnp.dot(tokens, weight, preferred_element_type=jnp.float32),
                        Layout(major_to_minor=(0, 1)),
                    )
                    for weight in (w_gate, w_up)
                ],
                axis=1,
            ),
            "kv",
            scatter_dimension=0,
            tiled=True,
        )
        local_hidden = (jax.nn.silu(gate_up[:, :hidden_cols]) * gate_up[:, hidden_cols:]).astype(
            jnp.bfloat16
        )
        hidden_all = gather_by_permute(local_hidden, "kv").reshape(-1, local_hidden.shape[1])
        residual = residual + scatter_sum(
            jnp.dot(hidden_all, w_down, preferred_element_type=jnp.float32), "req"
        )
    return residual


def solution(mesh):
    return jax.shard_map(
        body,
        mesh=mesh,
        in_specs=(
            P("req", "kv"),
            P(),
            P(),
            P(None, "req", "kv"),
            P(None, "req", "kv"),
            P("kv"),
            P("req", "kv"),
            P("req", "kv"),
            P("req", "kv"),
            P("kv"),
            P("kv"),
            P("kv"),
            P("req", "kv"),
            P("kv"),
            P("kv", "req"),
            P("kv", "req"),
            P("req", "kv"),
        ),
        out_specs=P("req", "kv"),
        check_vma=False,
    )
```

```python
import math

import jax
import jax.numpy as jnp
from jax import lax
from jax.sharding import PartitionSpec as P

MODEL_WIDTH = 8192
HEAD_SIZE = 128
LAYER_COUNT = 2


EPS = 1e-06
LOG_BASE = math.log(1000000.0)


def scatter_sum(block, axis):
    count = lax.axis_size(axis)
    index = lax.axis_index(axis)
    chunks = block.reshape(count, block.shape[0] // count, *block.shape[1:])
    if count % 2 or count == 2:
        total = jnp.take(chunks, index, axis=0)
        for shift in range(1, count):
            piece = jnp.take(chunks, (index + shift) % count, axis=0)
            total = total + lax.ppermute(
                piece, axis, [(j, (j + shift) % count) for j in range(count)]
            )
        return total
    half = count // 2
    parity = index % 2
    grouped = chunks.reshape(half, 2, *chunks.shape[1:])
    mine = jnp.take(grouped, parity, axis=1)
    theirs = jnp.take(grouped, 1 - parity, axis=1)
    partial = mine + lax.ppermute(theirs, axis, [(j, j ^ 1) for j in range(count)])
    group_index = index // 2
    total = jnp.take(partial, group_index, axis=0)
    for shift in range(1, half):
        piece = jnp.take(partial, (group_index + shift) % half, axis=0)
        pairs = [
            (2 * u + p, 2 * ((u + shift) % half) + p) for u in range(half) for p in range(2)
        ]
        total = total + lax.ppermute(piece, axis, pairs)
    return total


def gather_by_permute(block, axis):
    count = lax.axis_size(axis)
    index = lax.axis_index(axis)
    pieces = [block]
    for shift in range(1, count):
        pieces.append(
            lax.ppermute(block, axis, [(j, (j + shift) % count) for j in range(count)])
        )
    stacked = jnp.stack(pieces[:1] + pieces[1:][::-1])
    return jnp.roll(stacked, index, axis=0)


def rows_for_weights(block):
    req_size = lax.axis_size("req")
    kv_size = lax.axis_size("kv")
    ratio = req_size // kv_size
    rows, width = block.shape[0], block.shape[1] // ratio
    wide = gather_by_permute(block, "kv").reshape(kv_size, rows, ratio, width)
    wide = wide.transpose(0, 2, 1, 3).reshape(req_size * rows, width)
    return lax.all_to_all(wide, "req", 0, 0, tiled=True)


def apply_rotation(values, token_positions):
    half_width = values.shape[-1] // 2
    frequency = jnp.exp(
        -LOG_BASE * jnp.arange(half_width, dtype=jnp.float32) * 2.0 / values.shape[-1]
    )
    angles = token_positions[:, None] * frequency[None, :]
    reshape_to = (angles.shape[0],) + (1,) * (values.ndim - 2) + (half_width,)
    cosine = jnp.cos(angles).reshape(reshape_to)
    sine_part = jnp.sin(angles).reshape(reshape_to)
    front_half = values[..., :half_width]
    back_half = values[..., half_width:]
    return jnp.concatenate(
        [front_half * cosine - back_half * sine_part, back_half * cosine + front_half * sine_part],
        axis=-1,
    )


def normalize(residual, gains):
    square_sum = jnp.sum(residual * residual, axis=1)
    all_squares = lax.psum(square_sum, "kv")
    inv_norm = lax.rsqrt(all_squares / MODEL_WIDTH + EPS)
    return (residual * inv_norm[:, None] * gains.astype(jnp.float32)[None, :]).astype(jnp.bfloat16)


def attend(query_rows, fresh_key, fresh_value, key_cache, value_cache, layer, lengths):
    score_scale = 1.0 / math.sqrt(query_rows.shape[-1])
    requests, kv_heads, group, head_dim = query_rows.shape
    finish = jnp.cumsum(lengths)
    starts = finish - lengths
    capacity = key_cache.shape[1]
    key_rows = jnp.arange(capacity, dtype=jnp.int32)
    inside = (key_rows[None, :] >= starts[:, None]) & (key_rows[None, :] < finish[:, None])
    inside = jnp.broadcast_to(inside[:, None, :], (requests, group, capacity)).reshape(
        requests * group, capacity
    )
    outputs = []
    for head in range(kv_heads):
        columns = slice(head * head_dim, (head + 1) * head_dim)
        head_queries = query_rows[:, head].reshape(requests * group, head_dim)
        scores = (
            lax.dot_general(
                head_queries,
                key_cache[layer, :, columns],
                (((1,), (1,)), ((), ())),
                preferred_element_type=jnp.float32,
            )
            * score_scale
        )
        self_score = (
            jnp.einsum(
                "ird,id->ir",
                query_rows[:, head],
                fresh_key[:, head],
                preferred_element_type=jnp.float32,
            ).reshape(requests * group)
            * score_scale
        )
        top = jnp.maximum(jnp.max(jnp.where(inside, scores, -jnp.inf), axis=-1), self_score)
        exps = jnp.where(inside, jnp.exp(scores - top[:, None]), 0.0)
        self_exp = jnp.exp(self_score - top)
        total = jnp.sum(exps, axis=-1) + self_exp
        combined = jnp.dot(
            exps.astype(jnp.bfloat16),
            value_cache[layer, :, columns],
            preferred_element_type=jnp.float32,
        )
        fresh = jnp.repeat(fresh_value[:, head].astype(jnp.float32), group, axis=0)
        combined = combined + self_exp.astype(jnp.bfloat16).astype(jnp.float32)[:, None] * fresh
        outputs.append((combined / total[:, None]).astype(jnp.bfloat16).reshape(requests, group, head_dim))
    return jnp.stack(outputs, axis=1)


def body(
    hidden,
    cache_len,
    request_serving_order,
    rotated_key_cache,
    stored_value_cache,
    attn_gain,
    w_query,
    key_projection_weight,
    value_projection_weight,
    b_query,
    key_bias,
    value_bias,
    w_out,
    mlp_gain,
    w_gate,
    w_up,
    w_down,
):
    req_size = lax.axis_size("req")
    kv_size = lax.axis_size("kv")
    group_ratio = req_size // kv_size
    req_index = lax.axis_index("req")
    own_rows = hidden.shape[0]
    head_dim = HEAD_SIZE
    query_width = w_query.shape[1]
    key_width = key_projection_weight.shape[1]
    kv_heads = key_width // head_dim
    capacity = rotated_key_cache.shape[1]
    b_joint = jnp.concatenate([b_query, key_bias, value_bias]).astype(jnp.float32)
    request_count = request_serving_order.shape[0]
    inverse = jnp.sum(
        jnp.where(
            request_serving_order[:, None] == jnp.arange(request_count, dtype=jnp.int32)[None, :],
            jnp.arange(request_count, dtype=jnp.int32)[:, None],
            0,
        ),
        axis=0,
    )
    my_slots = lax.dynamic_slice_in_dim(request_serving_order, req_index * own_rows, own_rows)
    residual = hidden.astype(jnp.float32)
    for current_layer_index in range(LAYER_COUNT):
        normed = normalize(residual, attn_gain)
        columns = rows_for_weights(normed)
        picked = jnp.take(columns, request_serving_order, axis=0)
        combined = (
            scatter_sum(
                jnp.concatenate(
                    [
                        jnp.dot(picked, weight, preferred_element_type=jnp.float32)
                        for weight in (w_query, key_projection_weight, value_projection_weight)
                    ],
                    axis=1,
                ),
                "req",
            )
            + b_joint[None, :]
        )
        lengths = jnp.take(cache_len[current_layer_index], my_slots)
        token_positions = lengths.astype(jnp.float32)
        query_rows = apply_rotation(
            combined[:, :query_width].reshape(own_rows, kv_heads, -1, head_dim), token_positions
        ).astype(jnp.bfloat16)
        fresh_key = apply_rotation(
            combined[:, query_width : query_width + key_width].reshape(
                own_rows, kv_heads, head_dim
            ),
            token_positions,
        ).astype(jnp.bfloat16)
        fresh_value = (
            combined[:, query_width + key_width :]
            .reshape(own_rows, kv_heads, head_dim)
            .astype(jnp.bfloat16)
        )
        attention_output = attend(
            query_rows,
            fresh_key,
            fresh_value,
            rotated_key_cache,
            stored_value_cache,
            current_layer_index,
            lengths,
        ).reshape(own_rows, query_width)
        head_rows = rows_for_weights(attention_output)
        project_picked = jnp.take(head_rows, inverse, axis=0)
        residual = residual + scatter_sum(
            jnp.dot(project_picked, w_out, preferred_element_type=jnp.float32), "req"
        )
        normed_mlp = normalize(residual, mlp_gain)
        tokens = lax.all_gather(normed_mlp, "req", axis=0, tiled=True)
        hidden_cols = w_gate.shape[1]
        gate_up = lax.psum_scatter(
            jnp.concatenate(
                [
                    jnp.dot(tokens, w_gate, preferred_element_type=jnp.float32),
                    jnp.dot(tokens, w_up, preferred_element_type=jnp.float32),
                ],
                axis=1,
            ),
            "kv",
            scatter_dimension=0,
            tiled=True,
        )
        local_hidden = (jax.nn.silu(gate_up[:, :hidden_cols]) * gate_up[:, hidden_cols:]).astype(
            jnp.bfloat16
        )
        hidden_all = gather_by_permute(local_hidden, "kv").reshape(-1, local_hidden.shape[1])
        residual = residual + scatter_sum(
            jnp.dot(hidden_all, w_down, preferred_element_type=jnp.float32), "req"
        )
    return residual


def solution(mesh):
    return jax.shard_map(
        body,
        mesh=mesh,
        in_specs=(
            P("req", "kv"),
            P(),
            P(),
            P(None, "req", "kv"),
            P(None, "req", "kv"),
            P("kv"),
            P("req", "kv"),
            P("req", "kv"),
            P("req", "kv"),
            P("kv"),
            P("kv"),
            P("kv"),
            P("req", "kv"),
            P("kv"),
            P("kv", "req"),
            P("kv", "req"),
            P("req", "kv"),
        ),
        out_specs=P("req", "kv"),
        check_vma=False,
    )
```
